256 devices in a mesh: req: 32 (over z_hi, y, core), tp: 8 (over z_lo, x).
Axes of the slice: x: 4, y: 4, z: 8 (z_hi: 4, z_lo: 2; z = z_hi * 2 + z_lo), core: 2. Of those that a mesh axis runs over, the one named last changes fastest.
Arguments:
- hidden_states: bfloat16 [4096, 2880], P('req', 'tp'), may hold values from -64 to 64
- attn_gain: float32 [2880], replicated, may hold values from 0.1 to 1.9
- query_weight: bfloat16 [2880, 4096], P(None, 'tp'), may hold values from -0.109375 to 0.109375
- key_value_weight: bfloat16 [2880, 1024], P(None, 'tp'), may hold values from -0.3125 to 0.3125
- sink_logits: float32 [64], P('tp'), may hold values from 4 to 11
- prefix_cache: bfloat16 [32768, 1024], P('req', 'tp'), may hold values from -512 to 512
- out_weight: bfloat16 [4096, 2880], P('tp'), may hold values from -0.125 to 0.125
- ffn_gain: float32 [2880], replicated, may hold values from 0.1 to 1.9
- router_weight: bfloat16 [2880, 32], P('tp'), may hold values from -0.21875 to 0.21875
- gate_up_weight: bfloat16 [32, 2880, 2, 2880], P('req', None, None, 'tp'), may hold values from -0.4375 to 0.4375
- down_weight: bfloat16 [32, 2880, 2880], P('req', 'tp'), may hold values from -0.013671875 to 0.013671875
- route_ids: int32 [4096, 4], P('req'), may hold values from 0 to 31, all different within a row; in each aligned block of 128 rows (0 to 127, 128 to 255, ...) at most 24 rows name the same one
- prefix_group: int32 [32], replicated, may hold values from 0 to 1
- suffix_lengths: int32 [32], replicated, may hold values from 1 to 128, 2048 in all
Outputs:
- attn_out: bfloat16 [4096, 2880], P('req', 'tp')
- moe_out: bfloat16 [4096, 2880], P('req', 'tp')
The draws below stay inside these ranges and needn't reach their ends.
Inputs may be any that keep to these rules, and one draw needn't show every extreme that they name: `route_ids`: among the 128 tokens of one request no expert is named more than 24 times; some expert is named exactly 24 times in some requests. `suffix_lengths`: rows of a request from its length on are padding; the longest request fills all 128 slots.
All inputs are finite; a program needn't handle non-finite values.
Results may differ from the reference program's by a relative error of at most 0.02.
The reference program's roundings to bfloat16 on the way count: a program that leaves them out, or rounds other values in their place, can miss the bound.
Values may be sent and summed in bfloat16 or wider, within the bound.
No kernel may reach another device: no remote copies, remote signals or barrier semaphores. Data moves between devices by JAX's collectives and lax.ppermute only.
A program may use at most 128 MiB of HBM per device.

```python
import math
import jax
import jax.numpy as jnp
import numpy as np
from jax import lax

D = 2880
HEADS = 64
KV_HEADS = 8
HEAD = 64
FF = 2880
TOPK = 4
TOK_DEV = 128
EXPERTS = 32
CAP = 24
TOKENS = 4096
PLEN = 16384
N_REQ = 32
N_TP = 8


def draw_hidden_states(key, part):
    subkeys = jax.random.split(key, 3)
    column = jnp.arange(D, dtype=jnp.float32)[None, :]
    col_scale = jnp.exp(jax.random.uniform(subkeys[1], (1, D), jnp.float32, 0.0, math.log(10.0)) + math.log(3.0) * column / D)
    noise_part = jax.random.normal(subkeys[0], (TOKENS, D), jnp.float32)
    row_scale = jnp.exp(jax.random.uniform(subkeys[2], (TOKENS, 1), jnp.float32, 0.0, math.log(10.0)))
    return jnp.clip(0.2 * noise_part * row_scale * col_scale, -64.0, 64.0).astype(jnp.bfloat16)


def draw_prefix_cache(key, part):
    subkeys = jax.random.split(key, 1)
    width = KV_HEADS * 2 * HEAD
    row_count = 2 * PLEN
    is_key = jnp.arange(width, dtype=jnp.int32) % (2 * HEAD) < HEAD
    col_scale = jnp.where(is_key, 1.5, 1.0)[None, :]
    values = jax.random.normal(subkeys[0], (row_count, width), jnp.float32) * col_scale
    return jnp.clip(values, -512.0, 512.0).astype(jnp.bfloat16)


def set_ends(array, stream_key, least, largest):
    longest = array.shape.index(max(array.shape))
    spots = []
    for shift in (0, 1):
        where = [jax.random.randint(jax.random.fold_in(stream_key, axis), (), 0, length) for axis, length in enumerate(array.shape)]
        where[longest] = (where[longest] + shift) % array.shape[longest]
        spots.append(tuple(where))
    return array.at[spots[0]].set(least).at[spots[1]].set(largest)


def shard_levels(stream_key, dims, pieces, low, top_value):
    def one(dim, shards_of):
        draws = jax.random.uniform(jax.random.fold_in(jax.random.fold_in(stream_key, 6), dim), (shards_of,), jnp.float32, low / len(pieces), top_value / len(pieces))
        return jnp.repeat(jnp.exp(draws), dims[dim] // shards_of).reshape((-1,) + (1,) * (len(dims) - dim - 1))

    level = one(*pieces[0])
    for cut in pieces[1:]:
        level = level * one(*cut)
    return level


def length_profile(number_of, total, bound, lean):
    loads = [(1 << 20) // math.isqrt(rank ** lean) + 1 for rank in range(2, number_of + 1)]
    surplus, holding = total - bound - (number_of - 1), [1] * (number_of - 1)
    while surplus > 0:
        candidates = [i for i in range(number_of - 1) if holding[i] < bound]
        whole, remaining = sum([loads[i] for i in candidates]), surplus
        for i in candidates:
            extra = min(bound - holding[i], max(1, remaining * loads[i] // whole), surplus)
            holding[i] = holding[i] + extra
            surplus = surplus - extra
    return np.array([bound] + holding)


def uneven(own_key, amount, total, most, skew):
    if amount == 2:
        one = jax.random.randint(own_key, (), max(1, total - most), min(most, total - 1) + 1)
        return jnp.stack([one, total - one])
    tallies = jnp.asarray(length_profile(amount, total, most, skew), jnp.int32)
    pairs = (amount - 1) // 2
    giver, sink = tallies[1:1 + 2 * pairs:2], tallies[2:2 + 2 * pairs:2]
    margin = jnp.minimum(giver - 1, most - sink)
    passed = jax.random.randint(jax.random.fold_in(own_key, 1), (pairs,), 0, 1 << 20) % (margin + 1)
    tallies = tallies.at[1:1 + 2 * pairs:2].set(giver - passed).at[2:2 + 2 * pairs:2].set(sink + passed)
    return tallies[jax.random.permutation(jax.random.fold_in(own_key, 2), amount)]


def routed_block(key, own, number, rows, amount, top, most, slope):
    order = jax.random.permutation(key, amount)
    heavy_load, usual = shares(amount, rows * top, most, slope, True), shares(amount, rows * top, most, slope, False)
    places = jnp.arange(amount)

    def named(tallies, offset_by):
        used = int((tallies > 0).sum())
        fixed = max(1, used // 4)
        shifted = fixed + (places - fixed + offset_by * (used - fixed)) % max(1, amount - fixed)
        return jnp.zeros((amount,), jnp.int32).at[order[jnp.where(places < fixed, places, shifted)]].set(jnp.asarray(tallies, jnp.int32))

    tallies = jnp.where(number % 4 == 0, named(heavy_load, number // 4), named(usual, number - number // 4 - 1))
    mixed = jax.random.permutation(jax.random.fold_in(own, 3), amount)
    donor, sink = mixed[0:amount // 2 * 2:2], mixed[1:amount // 2 * 2:2]
    room = jnp.minimum(tallies[donor] - 1, most - tallies[sink]) // 2
    room = jnp.where((donor == order[0]) | (sink == order[0]) | (tallies[sink] == 0), 0, jnp.maximum(room, 0))
    shifted = jax.random.randint(jax.random.fold_in(own, 4), (amount // 2,), 0, 1 << 20) % (room + 1)
    tallies = tallies.at[donor].add(-shifted).at[sink].add(shifted)
    labels = jnp.searchsorted(jnp.cumsum(tallies), jnp.arange(rows * top), side="right").astype(jnp.int32)
    listing = labels.reshape(top, rows).T
    listing = listing[jax.random.permutation(jax.random.fold_in(own, 1), rows)]
    offset_by = jax.random.randint(jax.random.fold_in(own, 2), (rows, 1), 0, top)
    return jnp.take_along_axis(listing, (jnp.arange(top)[None, :] + offset_by) % top, axis=1)


def shares(amount, total, limit, lean, full):
    portions = [(1 << 20) // math.isqrt(rank ** lean) + 1 for rank in range(1, amount + 1)]
    largest = limit if full else min(limit, max(-(-total // amount), total * portions[0] // sum(portions)))
    least = 1 if total - largest >= amount - 1 else 0
    holding, spare = [largest] + [least] * (amount - 1), total - largest - least * (amount - 1)
    while spare > 0:
        free = [i for i in range(1, amount) if holding[i] < largest] or [i for i in range(1, amount) if holding[i] < limit]
        pool, left = sum([portions[i] for i in free]), spare
        for i in free:
            addition = min(limit - holding[i], max(1, left * portions[i] // pool), spare)
            holding[i] = holding[i] + addition
            spare = spare - addition
    return np.array(holding)


def bell_draw(rng, dims, scale, bound, shards=(), kind=jnp.bfloat16):
    drawn = scale * jax.random.normal(rng, dims, jnp.float32)
    if shards:
        drawn = drawn * shard_levels(rng, dims, shards, -0.22, 0.18)
    return jnp.clip(drawn, -bound, bound).astype(kind)


def setup_inputs(seed: int = 0) -> dict:
    key_list = jax.random.split(jax.random.key(seed), 15)
    hidden_states = draw_hidden_states(jax.random.fold_in(key_list[14], 71), 0)
    attn_gain = jnp.clip(1.0 + 0.18 * jax.random.normal(key_list[1], (D,), jnp.float32), 0.1, 1.9)
    query_weight = bell_draw(key_list[2], (D, HEADS * HEAD), D ** -0.5, 0.109375, ((1, 8),))
    key_value_weight = bell_draw(key_list[3], (D, KV_HEADS * 2 * HEAD), (D // 9) ** -0.5, 0.3125, ((1, 8),))
    sink_logits = jnp.clip(4.0 + 7.0 * jax.random.uniform(key_list[4], (HEADS,), jnp.float32) ** shard_levels(key_list[4], (HEADS,), ((0, 8),), -0.2, 0.2), 4.0, 11.0)
    prefix_cache = draw_prefix_cache(jax.random.fold_in(key_list[14], 71), 0)
    out_weight = bell_draw(key_list[6], (HEADS * HEAD, D), (HEADS * HEAD // 2) ** -0.5, 0.125, ((0, 8),))
    ffn_gain = jnp.clip(1.0 + 0.18 * jax.random.normal(key_list[7], (D,), jnp.float32), 0.1, 1.9)
    router_weight = bell_draw(key_list[8], (D, EXPERTS), (D // 4) ** -0.5, 0.21875, ((0, 8),))
    gate_up_weight = bell_draw(key_list[9], (EXPERTS, D, 2, FF), (D // 16) ** -0.5, 0.4375, ((0, 32), (3, 8)))
    down_weight = bell_draw(key_list[10], (EXPERTS, FF, D), (FF * 64) ** -0.5, 0.013671875, ((0, 32), (1, 8)))
    route_ids_keys = jax.random.split(jax.random.fold_in(key_list[11], 1), TOKENS // TOK_DEV)
    route_ids_turns = jax.random.permutation(jax.random.fold_in(key_list[11], 3), TOKENS // TOK_DEV)
    route_ids = jax.vmap(lambda own, number: routed_block(jax.random.fold_in(key_list[11], 2), own, number, TOK_DEV, EXPERTS, TOPK, CAP, 2))(route_ids_keys, route_ids_turns).reshape((TOKENS, TOPK))
    prefix_group = set_ends(jax.random.randint(key_list[12], (N_REQ,), 0, 2), jax.random.fold_in(key_list[12], 1), 0, 1).astype(jnp.int32)
    suffix_lengths = uneven(key_list[13], N_REQ, N_REQ * TOK_DEV // 2, TOK_DEV, 2).astype(jnp.int32)
    return dict(hidden_states=hidden_states, attn_gain=attn_gain, query_weight=query_weight, key_value_weight=key_value_weight, sink_logits=sink_logits, prefix_cache=prefix_cache, out_weight=out_weight, ffn_gain=ffn_gain, router_weight=router_weight, gate_up_weight=gate_up_weight, down_weight=down_weight, route_ids=route_ids, prefix_group=prefix_group, suffix_lengths=suffix_lengths)


rope_base = 150000.0
norm_eps = 1e-05
clamp_limit = 7.0
glu_alpha = 1.702

def rms_rows(values, gain):
    wide = values.astype(jnp.float32)
    factor = lax.rsqrt(lax.optimization_barrier(jnp.mean(wide * wide, axis=1, keepdims=True)) + norm_eps)
    return (wide * factor * gain).astype(jnp.bfloat16)

def rotate(values, positions):
    half_size = values.shape[-1] // 2
    powers = jnp.arange(half_size, dtype=jnp.float32) * (-2.0 / values.shape[-1])
    angles = positions[:, None, None] * rope_base ** powers
    cosine = jnp.cos(angles)
    sine_part = jnp.sin(angles)
    first_half = values[..., :half_size]
    second_half = values[..., half_size:]
    return jnp.concatenate([first_half * cosine - second_half * sine_part, second_half * cosine + first_half * sine_part], axis=-1)

def reference(hidden_states, attn_gain, query_weight, key_value_weight, sink_logits, prefix_cache, out_weight, ffn_gain, router_weight, gate_up_weight, down_weight, route_ids, prefix_group, suffix_lengths):
    per_kv = HEADS // KV_HEADS
    query_rows = per_kv * TOK_DEV
    score_scale = HEAD ** (-0.5)
    normed_attn = rms_rows(hidden_states, attn_gain)
    positions = (PLEN + jnp.arange(TOKENS, dtype=jnp.int32) % TOK_DEV).astype(jnp.float32)
    queries = jnp.dot(normed_attn, query_weight, preferred_element_type=jnp.float32).reshape(TOKENS, HEADS, HEAD)
    fresh = jnp.dot(normed_attn, key_value_weight, preferred_element_type=jnp.float32).reshape(TOKENS, KV_HEADS, 2, HEAD)
    queries = rotate(queries, positions).astype(jnp.bfloat16)
    new_keys = rotate(fresh[:, :, 0], positions).astype(jnp.bfloat16)
    new_values = fresh[:, :, 1].astype(jnp.bfloat16)
    causal = jnp.arange(TOK_DEV, dtype=jnp.int32)[None, :] <= (jnp.arange(query_rows, dtype=jnp.int32) % TOK_DEV)[:, None]
    keep_mask = jnp.concatenate([jnp.ones((query_rows, PLEN), jnp.bool_), causal], axis=1)
    head_sink = sink_logits.reshape(KV_HEADS, per_kv)

    def per_request(request):
        row_start = request * TOK_DEV
        group_start = prefix_group[request] * PLEN
        req_q = lax.dynamic_slice_in_dim(queries, row_start, TOK_DEV, 0)
        req_k = lax.dynamic_slice_in_dim(new_keys, row_start, TOK_DEV, 0)
        req_v = lax.dynamic_slice_in_dim(new_values, row_start, TOK_DEV, 0)
        prefix_rows = lax.dynamic_slice_in_dim(prefix_cache, group_start, PLEN, 0).reshape(PLEN, KV_HEADS, 2, HEAD)
        head_q = req_q.reshape(TOK_DEV, KV_HEADS, per_kv, HEAD).transpose(1, 2, 0, 3).reshape(KV_HEADS, query_rows, HEAD)
        head_k = jnp.concatenate([prefix_rows[:, :, 0], req_k], axis=0).transpose(1, 0, 2)
        head_v = jnp.concatenate([prefix_rows[:, :, 1], req_v], axis=0).transpose(1, 0, 2)

        def attend(head_item):
            q_rows, k_rows, v_rows, sink_row = head_item
            scores = jnp.dot(q_rows, k_rows.T, preferred_element_type=jnp.float32) * score_scale
            scores = jnp.where(keep_mask, scores, -jnp.inf)
            sink_col = jnp.repeat(sink_row, TOK_DEV)
            peak = jnp.maximum(sink_col, lax.optimization_barrier(jnp.max(scores, axis=1)))
            weights = jnp.exp(scores - peak[:, None])
            denominator = jnp.exp(sink_col - peak) + lax.optimization_barrier(jnp.sum(weights, axis=1))
            mixed_rows = jnp.dot(weights.astype(jnp.bfloat16), v_rows, preferred_element_type=jnp.float32) / denominator[:, None]
            return mixed_rows.astype(jnp.bfloat16)
        mixed_heads = lax.map(attend, (head_q, head_k, head_v, head_sink))
        return mixed_heads.reshape(KV_HEADS, per_kv, TOK_DEV, HEAD).transpose(2, 0, 1, 3).reshape(TOK_DEV, HEADS * HEAD)
    mixed = lax.map(per_request, jnp.arange(N_REQ, dtype=jnp.int32)).reshape(TOKENS, HEADS * HEAD)
    attn_sum = jnp.dot(mixed, out_weight, preferred_element_type=jnp.float32)
    live = (jnp.arange(TOKENS, dtype=jnp.int32) % TOK_DEV < jnp.repeat(suffix_lengths, TOK_DEV))[:, None]
    attn_out = jnp.where(live, attn_sum, 0.0).astype(jnp.bfloat16)
    resid = (hidden_states.astype(jnp.float32) + attn_sum).astype(jnp.bfloat16)
    normed_ffn = rms_rows(resid, ffn_gain)
    logits = jnp.dot(normed_ffn, router_weight, preferred_element_type=jnp.float32)
    chosen = jnp.take_along_axis(logits, route_ids, axis=1)
    raised = jnp.exp(chosen)
    gates = raised / lax.optimization_barrier(jnp.sum(raised, axis=1, keepdims=True))
    entries = route_ids.reshape(N_REQ, TOK_DEV * TOPK)
    onehot = (entries[:, :, None] == jnp.arange(EXPERTS, dtype=jnp.int32)[None, None, :]).astype(jnp.int32)
    earlier = jnp.cumsum(onehot, axis=1) - onehot
    slots = lax.optimization_barrier(jnp.sum(earlier * onehot, axis=2))
    targets = (entries * (N_REQ * CAP) + jnp.arange(N_REQ, dtype=jnp.int32)[:, None] * CAP + slots).reshape(-1)
    owner_token = jnp.arange(TOKENS * TOPK, dtype=jnp.int32) // TOPK
    table = jnp.zeros((EXPERTS * N_REQ * CAP,), jnp.int32).at[targets].set(owner_token)
    filled = jnp.zeros((EXPERTS * N_REQ * CAP,), jnp.bool_).at[targets].set(True)
    ff_part = FF // N_TP

    def expert(expert_item):
        table_rows, fill_rows, gate_up, down_rows = expert_item
        rows = jnp.where(fill_rows[:, None], normed_ffn[table_rows], jnp.zeros((), jnp.bfloat16))
        gate_value = jnp.minimum(jnp.dot(rows, gate_up[:, 0, :], preferred_element_type=jnp.float32), clamp_limit)
        up_value = jnp.clip(jnp.dot(rows, gate_up[:, 1, :], preferred_element_type=jnp.float32), -clamp_limit, clamp_limit)
        active = ((up_value + 1.0) * gate_value * jax.nn.sigmoid(glu_alpha * gate_value)).astype(jnp.bfloat16)
        total_rows = jnp.zeros((N_REQ * CAP, D), jnp.float32)
        for group_index in range(N_TP):
            lower = group_index * ff_part
            partial_rows = jnp.dot(active[:, lower:lower + ff_part], down_rows[lower:lower + ff_part], preferred_element_type=jnp.float32)
            total_rows = total_rows + lax.optimization_barrier(partial_rows.astype(jnp.bfloat16)).astype(jnp.float32)
        return total_rows
    expert_result = lax.map(expert, (table.reshape(EXPERTS, N_REQ * CAP), filled.reshape(EXPERTS, N_REQ * CAP), gate_up_weight, down_weight))
    picked = expert_result.reshape(EXPERTS * N_REQ * CAP, D)[targets].reshape(TOKENS, TOPK, D)
    moe_sum = lax.optimization_barrier(jnp.sum(picked * gates[:, :, None], axis=1))
    moe_out = jnp.where(live, moe_sum, 0.0).astype(jnp.bfloat16)
    return (attn_out, moe_out)
```

```python
import functools

import jax
import jax.numpy as jnp
from jax import lax
from jax.experimental import pallas as pl
from jax.experimental.pallas import tpu as pltpu
from jax.sharding import PartitionSpec as P

D = 2880
HEAD = 64


rope_base = 150000.0
norm_eps = 1e-05
clamp_limit = 7.0
glu_alpha = 1.702


def rms_rows(values, gain):
    wide = values.astype(jnp.float32)
    factor = lax.rsqrt(jnp.mean(wide * wide, axis=1, keepdims=True) + norm_eps)
    return (wide * factor * gain).astype(jnp.bfloat16)


def rotate(values, positions):
    half_size = values.shape[-1] // 2
    powers = jnp.arange(half_size, dtype=jnp.float32) * (-2.0 / values.shape[-1])
    angles = positions[:, None, None] * rope_base**powers
    cosine = jnp.cos(angles)
    sine_part = jnp.sin(angles)
    first_half = values[..., :half_size]
    second_half = values[..., half_size:]
    return jnp.concatenate(
        [
            first_half * cosine - second_half * sine_part,
            second_half * cosine + first_half * sine_part,
        ],
        axis=-1,
    )


def flash_kernel(group_ref, q_ref, kv_ref, m0_ref, l0_ref, acc0_ref, out_ref, m_sc, l_sc, acc_sc, *, scale, steps):
    step = pl.program_id(1)

    @pl.when(step == 0)
    def _():
        m_sc[...] = m0_ref[...]
        l_sc[...] = l0_ref[...]
        acc_sc[...] = acc0_ref[...]

    block = kv_ref[...]
    scores = (
        lax.dot_general(
            q_ref[...], block, (((1,), (1,)), ((), ())), preferred_element_type=jnp.float32
        )
        * scale
    )
    m_prev = m_sc[...]
    m_new = jnp.maximum(m_prev, jnp.max(scores, axis=1, keepdims=True))
    weights = jnp.exp(scores - m_new)
    decay = jnp.exp(m_prev - m_new)
    l_sc[...] = decay * l_sc[...] + jnp.sum(weights, axis=1, keepdims=True)
    acc_sc[...] = decay * acc_sc[...] + jnp.dot(
        weights.astype(jnp.bfloat16), block, preferred_element_type=jnp.float32
    )
    m_sc[...] = m_new

    @pl.when(step == steps - 1)
    def _():
        out_ref[...] = (acc_sc[...] / l_sc[...]).astype(out_ref.dtype)


def prefix_attention(group, query, cache, peak, denominator, accum, *, prefix_len, scale):
    rows, width = query.shape
    block_q = min(rows, 1024)
    block_k = 1024
    steps = prefix_len // block_k
    grid = (rows // block_q, steps)
    kernel = functools.partial(flash_kernel, scale=scale, steps=steps)
    return pl.pallas_call(
        kernel,
        out_shape=jax.ShapeDtypeStruct((rows, width), jnp.bfloat16),
        grid_spec=pltpu.PrefetchScalarGridSpec(
            num_scalar_prefetch=1,
            grid=grid,
            in_specs=[
                pl.BlockSpec((block_q, width), lambda i, j, g: (i, 0)),
                pl.BlockSpec((block_k, width), lambda i, j, g: (g[0] * steps + j, 0)),
                pl.BlockSpec((block_q, 1), lambda i, j, g: (i, 0)),
                pl.BlockSpec((block_q, 1), lambda i, j, g: (i, 0)),
                pl.BlockSpec((block_q, width), lambda i, j, g: (i, 0)),
            ],
            out_specs=pl.BlockSpec((block_q, width), lambda i, j, g: (i, 0)),
            scratch_shapes=[
                pltpu.VMEM((block_q, 1), jnp.float32),
                pltpu.VMEM((block_q, 1), jnp.float32),
                pltpu.VMEM((block_q, width), jnp.float32),
            ],
        ),
        compiler_params=pltpu.CompilerParams(dimension_semantics=("arbitrary", "arbitrary")),
        cost_estimate=pl.CostEstimate(
            flops=4 * rows * prefix_len * width,
            transcendentals=rows * prefix_len,
            bytes_accessed=prefix_len * width * 2 + rows * width * 8,
        ),
    )(group, query, cache, peak, denominator, accum)


def local(
    hidden_states,
    attn_gain,
    query_weight,
    key_value_weight,
    sink_logits,
    prefix_cache,
    out_weight,
    ffn_gain,
    router_weight,
    gate_up_weight,
    down_weight,
    route_ids,
    prefix_group,
    suffix_lengths,
):
    token_count = hidden_states.shape[0]
    head_size = HEAD
    model_width = D
    local_heads = query_weight.shape[1] // head_size
    local_kv = key_value_weight.shape[1] // (2 * head_size)
    per_kv = local_heads // local_kv
    query_rows = per_kv * token_count
    req_count = lax.axis_size("req")
    req_index = lax.axis_index("req")
    tp_index = lax.axis_index("tp")
    cache_rows = prefix_cache.shape[0]
    prefix_len = cache_rows * req_count // 2
    score_scale = head_size ** (-0.5)
    router_full = lax.all_gather(router_weight, "tp", axis=0, tiled=True)
    full_rows = lax.all_gather(hidden_states, "tp", axis=1, tiled=True)
    normed_attn = rms_rows(full_rows, attn_gain)
    positions = (prefix_len + jnp.arange(token_count, dtype=jnp.int32)).astype(jnp.float32)
    queries = jnp.dot(normed_attn, query_weight, preferred_element_type=jnp.float32)
    fresh = jnp.dot(normed_attn, key_value_weight, preferred_element_type=jnp.float32).reshape(
        token_count, local_kv, 2, head_size
    )
    queries = rotate(queries.reshape(token_count, local_heads, head_size), positions).astype(
        jnp.bfloat16
    )
    new_keys = rotate(fresh[:, :, 0], positions).astype(jnp.bfloat16)
    new_values = fresh[:, :, 1].astype(jnp.bfloat16)
    query_heads = (
        queries.reshape(token_count, local_kv, per_kv, head_size)
        .transpose(1, 2, 0, 3)
        .reshape(local_kv, query_rows, head_size)
    )
    assert local_kv == 1
    query_flat = query_heads.reshape(query_rows, head_size)
    fresh_kv = jnp.concatenate([new_keys[:, 0, :], new_values[:, 0, :]], axis=1)
    sink_rows = jnp.broadcast_to(
        sink_logits.reshape(per_kv, 1), (per_kv, token_count)
    ).reshape(query_rows, 1)
    row_pos = jnp.arange(query_rows, dtype=jnp.int32) % token_count
    causal = jnp.arange(token_count, dtype=jnp.int32)[None, :] <= row_pos[:, None]
    fresh_scores = (
        jnp.dot(query_flat, new_keys[:, 0, :].T, preferred_element_type=jnp.float32) * score_scale
    )
    fresh_scores = jnp.where(causal, fresh_scores, -jnp.inf)
    start_peak = jnp.maximum(sink_rows, jnp.max(fresh_scores, axis=1, keepdims=True))
    fresh_weights = jnp.exp(fresh_scores - start_peak)
    start_denominator = jnp.exp(sink_rows - start_peak) + jnp.sum(
        fresh_weights, axis=1, keepdims=True
    )
    start_accum = jnp.dot(
        fresh_weights.astype(jnp.bfloat16), fresh_kv, preferred_element_type=jnp.float32
    )
    query_padded = jnp.concatenate([query_flat, jnp.zeros_like(query_flat)], axis=1)
    own_group = prefix_group[req_index].reshape(1)
    shard_rows = lax.all_gather(prefix_cache, "req", axis=0, tiled=True)
    mixed_wide = prefix_attention(
        own_group, query_padded, shard_rows, start_peak, start_denominator, start_accum,
        prefix_len=prefix_len, scale=score_scale,
    )
    mixed = mixed_wide[:, head_size:].reshape(local_heads, token_count, head_size)
    attn_part = jnp.einsum(
        "hqd,hdo->qo",
        mixed,
        out_weight.reshape(local_heads, head_size, model_width),
        preferred_element_type=jnp.float32,
    )
    attn_sum = lax.psum_scatter(attn_part, "tp", scatter_dimension=1, tiled=True)
    col_count = attn_sum.shape[1]
    live = (jnp.arange(token_count, dtype=jnp.int32) < suffix_lengths[req_index])[:, None]
    attn_out = jnp.where(live, attn_sum, 0.0).astype(jnp.bfloat16)
    resid = (hidden_states.astype(jnp.float32) + attn_sum).astype(jnp.bfloat16)
    expert_count = router_weight.shape[1]
    top_count = route_ids.shape[1]
    capacity = token_count * top_count * 3 // (2 * expert_count)
    entries = route_ids.reshape(-1)
    onehot = (entries[:, None] == jnp.arange(expert_count, dtype=jnp.int32)[None, :]).astype(
        jnp.int32
    )
    earlier = jnp.cumsum(onehot, axis=0) - onehot
    slots = jnp.sum(earlier * onehot, axis=1)
    targets = entries * capacity + slots
    sources = jnp.arange(token_count * top_count, dtype=jnp.int32) // top_count
    source_of = jnp.zeros((expert_count * capacity,), jnp.int32).at[targets].set(sources)
    filled = jnp.zeros((expert_count * capacity,), jnp.bool_).at[targets].set(True)
    exp_local = gate_up_weight.shape[0]
    ff_local = gate_up_weight.shape[3]
    joined_weight = gate_up_weight.reshape(exp_local, model_width, 2 * ff_local)
    resid_rows = lax.all_gather(resid, "tp", axis=1, tiled=True)
    normed_rows = rms_rows(resid_rows, ffn_gain)
    picked_rows = jnp.where(filled[:, None], normed_rows[source_of], jnp.zeros((), jnp.bfloat16))
    arrived = lax.all_to_all(
        picked_rows.reshape(expert_count, capacity, normed_rows.shape[1]),
        "req",
        split_axis=0,
        concat_axis=0,
        tiled=True,
    )
    item_count = arrived.shape[1]
    grouped = arrived.reshape(req_count, exp_local, item_count, model_width)
    projected = jnp.einsum(
        "sepd,edf->sepf", grouped, joined_weight, preferred_element_type=jnp.float32
    )
    gate_value = jnp.minimum(projected[..., :ff_local], clamp_limit)
    up_value = jnp.clip(projected[..., ff_local:], -clamp_limit, clamp_limit)
    active = ((up_value + 1.0) * gate_value * jax.nn.sigmoid(glu_alpha * gate_value)).astype(
        jnp.bfloat16
    )
    results = jnp.einsum(
        "sepf,efd->sepd", active, down_weight, preferred_element_type=jnp.float32
    ).astype(jnp.bfloat16)
    send_results = results.reshape(arrived.shape[0], item_count, model_width)
    returned = lax.all_to_all(send_results, "req", split_axis=0, concat_axis=0, tiled=True)
    logits = jnp.dot(normed_rows, router_full, preferred_element_type=jnp.float32)
    chosen = jnp.take_along_axis(logits, route_ids, axis=1)
    raised = jnp.exp(chosen)
    gates = raised / jnp.sum(raised, axis=1, keepdims=True)
    picked_back = returned.reshape(expert_count * capacity, model_width)[targets]
    combined = jnp.sum(
        picked_back.reshape(token_count, top_count, model_width).astype(jnp.float32)
        * gates[:, :, None],
        axis=1,
    )
    moe_sum = lax.psum_scatter(combined, "tp", scatter_dimension=1, tiled=True)
    moe_out = jnp.where(live, moe_sum, 0.0).astype(jnp.bfloat16)
    return (attn_out, moe_out)


def solution(mesh):
    return jax.shard_map(
        local,
        mesh=mesh,
        in_specs=(
            P("req", "tp"),
            P(),
            P(None, "tp"),
            P(None, "tp"),
            P("tp"),
            P("req", "tp"),
            P("tp", None),
            P(),
            P("tp", None),
            P("req", None, None, "tp"),
            P("req", "tp", None),
            P("req", None),
            P(),
            P(),
        ),
        out_specs=(P("req", "tp"), P("req", "tp")),
        check_vma=False,
    )
```

```python
import functools

import jax
import jax.numpy as jnp
from jax import lax
from jax.experimental import pallas as pl
from jax.experimental.pallas import tpu as pltpu
from jax.sharding import PartitionSpec as P

D = 2880
HEAD = 64


rope_base = 150000.0
norm_eps = 1e-05
clamp_limit = 7.0
glu_alpha = 1.702


def rms_rows(values, gain):
    wide = values.astype(jnp.float32)
    factor = lax.rsqrt(jnp.mean(wide * wide, axis=1, keepdims=True) + norm_eps)
    return (wide * factor * gain).astype(jnp.bfloat16)


def rotate(values, positions):
    half_size = values.shape[-1] // 2
    powers = jnp.arange(half_size, dtype=jnp.float32) * (-2.0 / values.shape[-1])
    angles = positions[:, None, None] * rope_base**powers
    cosine = jnp.cos(angles)
    sine_part = jnp.sin(angles)
    first_half = values[..., :half_size]
    second_half = values[..., half_size:]
    return jnp.concatenate(
        [
            first_half * cosine - second_half * sine_part,
            second_half * cosine + first_half * sine_part,
        ],
        axis=-1,
    )


def flash_kernel(group_ref, q_ref, kv_ref, m0_ref, l0_ref, acc0_ref, m_out, l_out, acc_out, m_sc, l_sc, acc_sc, *, scale, steps):
    step = pl.program_id(1)

    @pl.when(step == 0)
    def _():
        m_sc[...] = m0_ref[...]
        l_sc[...] = l0_ref[...]
        acc_sc[...] = acc0_ref[...]

    block = kv_ref[...]
    scores = (
        lax.dot_general(
            q_ref[...], block, (((1,), (1,)), ((), ())), preferred_element_type=jnp.float32
        )
        * scale
    )
    m_prev = m_sc[...]
    m_new = jnp.maximum(m_prev, jnp.max(scores, axis=1, keepdims=True))
    weights = jnp.exp(scores - m_new)
    decay = jnp.exp(m_prev - m_new)
    l_sc[...] = decay * l_sc[...] + jnp.sum(weights, axis=1, keepdims=True)
    acc_sc[...] = decay * acc_sc[...] + jnp.dot(
        weights.astype(jnp.bfloat16), block, preferred_element_type=jnp.float32
    )
    m_sc[...] = m_new

    @pl.when(step == steps - 1)
    def _():
        m_out[...] = m_sc[...]
        l_out[...] = l_sc[...]
        acc_out[...] = acc_sc[...]


def prefix_attention(group, query, cache, peak, denominator, accum, *, group_rows, scale):
    rows, width = query.shape
    block_q = min(rows, 1024)
    block_k = min(group_rows, 1024)
    steps = group_rows // block_k
    grid = (rows // block_q, steps)
    kernel = functools.partial(flash_kernel, scale=scale, steps=steps)
    row_spec = pl.BlockSpec((block_q, 1), lambda i, j, g: (i, 0))
    wide_spec = pl.BlockSpec((block_q, width), lambda i, j, g: (i, 0))
    return pl.pallas_call(
        kernel,
        out_shape=(
            jax.ShapeDtypeStruct((rows, 1), jnp.float32),
            jax.ShapeDtypeStruct((rows, 1), jnp.float32),
            jax.ShapeDtypeStruct((rows, width), jnp.float32),
        ),
        grid_spec=pltpu.PrefetchScalarGridSpec(
            num_scalar_prefetch=1,
            grid=grid,
            in_specs=[
                wide_spec,
                pl.BlockSpec((block_k, width), lambda i, j, g: (g[0] * steps + j, 0)),
                row_spec,
                row_spec,
                wide_spec,
            ],
            out_specs=[row_spec, row_spec, wide_spec],
            scratch_shapes=[
                pltpu.VMEM((block_q, 1), jnp.float32),
                pltpu.VMEM((block_q, 1), jnp.float32),
                pltpu.VMEM((block_q, width), jnp.float32),
            ],
        ),
        compiler_params=pltpu.CompilerParams(dimension_semantics=("arbitrary", "arbitrary")),
        cost_estimate=pl.CostEstimate(
            flops=4 * rows * group_rows * width,
            transcendentals=rows * group_rows,
            bytes_accessed=group_rows * width * 2 + rows * width * 10,
        ),
    )(group, query, cache, peak, denominator, accum)


def local(
    hidden_states,
    attn_gain,
    query_weight,
    key_value_weight,
    sink_logits,
    prefix_cache,
    out_weight,
    ffn_gain,
    router_weight,
    gate_up_weight,
    down_weight,
    route_ids,
    prefix_group,
    suffix_lengths,
):
    token_count = hidden_states.shape[0]
    head_size = HEAD
    model_width = D
    local_heads = query_weight.shape[1] // head_size
    local_kv = key_value_weight.shape[1] // (2 * head_size)
    per_kv = local_heads // local_kv
    query_rows = per_kv * token_count
    req_count = lax.axis_size("req")
    req_index = lax.axis_index("req")
    tp_index = lax.axis_index("tp")
    cache_rows = prefix_cache.shape[0]
    prefix_len = cache_rows * req_count // 2
    score_scale = head_size ** (-0.5)
    full_rows = lax.all_gather(hidden_states.T, "tp", axis=0, tiled=True).T
    router_full = lax.all_gather(router_weight, "tp", axis=0, tiled=True)
    full_rows, router_full = lax.optimization_barrier((full_rows, router_full))
    normed_attn = rms_rows(full_rows, attn_gain)
    positions = (prefix_len + jnp.arange(token_count, dtype=jnp.int32)).astype(jnp.float32)
    queries = jnp.dot(normed_attn, query_weight, preferred_element_type=jnp.float32)
    fresh = jnp.dot(normed_attn, key_value_weight, preferred_element_type=jnp.float32).reshape(
        token_count, local_kv, 2, head_size
    )
    queries = rotate(queries.reshape(token_count, local_heads, head_size), positions).astype(
        jnp.bfloat16
    )
    new_keys = rotate(fresh[:, :, 0], positions).astype(jnp.bfloat16)
    new_values = fresh[:, :, 1].astype(jnp.bfloat16)
    query_heads = (
        queries.reshape(token_count, local_kv, per_kv, head_size)
        .transpose(1, 2, 0, 3)
        .reshape(local_kv, query_rows, head_size)
    )
    assert local_kv == 1
    query_flat = query_heads.reshape(query_rows, head_size)
    fresh_kv = jnp.concatenate([new_keys[:, 0, :], new_values[:, 0, :]], axis=1)
    sink_rows = jnp.broadcast_to(
        sink_logits.reshape(per_kv, 1), (per_kv, token_count)
    ).reshape(query_rows, 1)
    row_pos = jnp.arange(query_rows, dtype=jnp.int32) % token_count
    causal = jnp.arange(token_count, dtype=jnp.int32)[None, :] <= row_pos[:, None]
    fresh_scores = (
        jnp.dot(query_flat, new_keys[:, 0, :].T, preferred_element_type=jnp.float32) * score_scale
    )
    fresh_scores = jnp.where(causal, fresh_scores, -jnp.inf)
    start_peak = jnp.maximum(sink_rows, jnp.max(fresh_scores, axis=1, keepdims=True))
    fresh_weights = jnp.exp(fresh_scores - start_peak)
    start_denominator = jnp.exp(sink_rows - start_peak) + jnp.sum(
        fresh_weights, axis=1, keepdims=True
    )
    start_accum = jnp.dot(
        fresh_weights.astype(jnp.bfloat16), fresh_kv, preferred_element_type=jnp.float32
    )
    query_padded = jnp.concatenate([query_flat, jnp.zeros_like(query_flat)], axis=1)
    own_group = prefix_group[req_index].reshape(1)
    chunks = 4
    piece = cache_rows // chunks
    state = (start_peak, start_denominator, start_accum)
    for chunk in range(chunks):
        shard_rows = lax.all_gather(
            prefix_cache[chunk * piece:(chunk + 1) * piece], "req", axis=0, tiled=True
        )
        state = prefix_attention(
            own_group, query_padded, shard_rows, *state,
            group_rows=prefix_len // chunks, scale=score_scale,
        )
    final_peak, final_denominator, final_accum = state
    mixed_wide = (final_accum / final_denominator).astype(jnp.bfloat16)
    mixed = mixed_wide[:, head_size:].reshape(local_heads, token_count, head_size)
    attn_part = jnp.einsum(
        "hqd,hdo->qo",
        mixed,
        out_weight.reshape(local_heads, head_size, model_width),
        preferred_element_type=jnp.float32,
    )
    attn_sum = lax.psum_scatter(attn_part, "tp", scatter_dimension=1, tiled=True)
    col_count = attn_sum.shape[1]
    live = (jnp.arange(token_count, dtype=jnp.int32) < suffix_lengths[req_index])[:, None]
    attn_out = jnp.where(live, attn_sum, 0.0).astype(jnp.bfloat16)
    resid = (hidden_states.astype(jnp.float32) + attn_sum).astype(jnp.bfloat16)
    expert_count = router_weight.shape[1]
    top_count = route_ids.shape[1]
    capacity = token_count * top_count * 3 // (2 * expert_count)
    entries = route_ids.reshape(-1)
    onehot = (entries[:, None] == jnp.arange(expert_count, dtype=jnp.int32)[None, :]).astype(
        jnp.int32
    )
    earlier = jnp.cumsum(onehot, axis=0) - onehot
    slots = jnp.sum(earlier * onehot, axis=1)
    targets = entries * capacity + slots
    sources = jnp.arange(token_count * top_count, dtype=jnp.int32) // top_count
    source_of = jnp.zeros((expert_count * capacity,), jnp.int32).at[targets].set(sources)
    filled = jnp.zeros((expert_count * capacity,), jnp.bool_).at[targets].set(True)
    exp_local = gate_up_weight.shape[0]
    ff_local = gate_up_weight.shape[3]
    joined_weight = gate_up_weight.reshape(exp_local, model_width, 2 * ff_local)
    resid_rows = lax.all_gather(resid.T, "tp", axis=0, tiled=True).T
    normed_rows = rms_rows(resid_rows, ffn_gain)
    picked_rows = jnp.where(filled[:, None], normed_rows[source_of], jnp.zeros((), jnp.bfloat16))
    arrived = lax.all_to_all(
        picked_rows.reshape(expert_count, capacity, normed_rows.shape[1]),
        "req",
        split_axis=0,
        concat_axis=0,
        tiled=True,
    )
    item_count = arrived.shape[1]
    grouped = arrived.reshape(req_count, exp_local, item_count, model_width)
    projected = jnp.einsum(
        "sepd,edf->sepf", grouped, joined_weight, preferred_element_type=jnp.float32
    )
    gate_value = jnp.minimum(projected[..., :ff_local], clamp_limit)
    up_value = jnp.clip(projected[..., ff_local:], -clamp_limit, clamp_limit)
    active = ((up_value + 1.0) * gate_value * jax.nn.sigmoid(glu_alpha * gate_value)).astype(
        jnp.bfloat16
    )
    results = jnp.einsum(
        "sepf,efd->sepd", active, down_weight, preferred_element_type=jnp.float32
    ).astype(jnp.bfloat16)
    send_results = results.reshape(arrived.shape[0], item_count, model_width)
    returned = lax.all_to_all(send_results, "req", split_axis=0, concat_axis=0, tiled=True)
    logits = jnp.dot(normed_rows, router_full, preferred_element_type=jnp.float32)
    chosen = jnp.take_along_axis(logits, route_ids, axis=1)
    raised = jnp.exp(chosen)
    gates = raised / jnp.sum(raised, axis=1, keepdims=True)
    picked_back = returned.reshape(expert_count * capacity, model_width)[targets]
    combined = jnp.sum(
        picked_back.reshape(token_count, top_count, model_width).astype(jnp.float32)
        * gates[:, :, None],
        axis=1,
    )
    moe_sum = lax.psum_scatter(combined, "tp", scatter_dimension=1, tiled=True)
    moe_out = jnp.where(live, moe_sum, 0.0).astype(jnp.bfloat16)
    return (attn_out, moe_out)


def solution(mesh):
    return jax.shard_map(
        local,
        mesh=mesh,
        in_specs=(
            P("req", "tp"),
            P(),
            P(None, "tp"),
            P(None, "tp"),
            P("tp"),
            P("req", "tp"),
            P("tp", None),
            P(),
            P("tp", None),
            P("req", None, None, "tp"),
            P("req", "tp", None),
            P("req", None),
            P(),
            P(),
        ),
        out_specs=(P("req", "tp"), P("req", "tp")),
        check_vma=False,
    )
```

```python
import functools

import jax
import jax.numpy as jnp
from jax import lax
from jax.experimental import pallas as pl
from jax.experimental.pallas import tpu as pltpu
from jax.sharding import PartitionSpec as P

D = 2880
HEAD = 64


rope_base = 150000.0
norm_eps = 1e-05
clamp_limit = 7.0
glu_alpha = 1.702


def rms_rows(values, gain):
    wide = values.astype(jnp.float32)
    factor = lax.rsqrt(jnp.mean(wide * wide, axis=1, keepdims=True) + norm_eps)
    return (wide * factor * gain).astype(jnp.bfloat16)


def rotate(values, positions):
    half_size = values.shape[-1] // 2
    powers = jnp.arange(half_size, dtype=jnp.float32) * (-2.0 / values.shape[-1])
    angles = positions[:, None, None] * rope_base**powers
    cosine = jnp.cos(angles)
    sine_part = jnp.sin(angles)
    first_half = values[..., :half_size]
    second_half = values[..., half_size:]
    return jnp.concatenate(
        [
            first_half * cosine - second_half * sine_part,
            second_half * cosine + first_half * sine_part,
        ],
        axis=-1,
    )


def flash_kernel(group_ref, q_ref, kv_ref, m0_ref, l0_ref, acc0_ref, out_ref, m_sc, l_sc, acc_sc, *, scale, steps):
    step = pl.program_id(1)

    @pl.when(step == 0)
    def _():
        m_sc[...] = m0_ref[...]
        l_sc[...] = l0_ref[...]
        acc_sc[...] = acc0_ref[...]

    block = kv_ref[...]
    scores = (
        lax.dot_general(
            q_ref[...], block, (((1,), (1,)), ((), ())), preferred_element_type=jnp.float32
        )
        * scale
    )
    m_prev = m_sc[...]
    m_new = jnp.maximum(m_prev, jnp.max(scores, axis=1, keepdims=True))
    weights = jnp.exp(scores - m_new)
    decay = jnp.exp(m_prev - m_new)
    l_sc[...] = decay * l_sc[...] + jnp.sum(weights, axis=1, keepdims=True)
    acc_sc[...] = decay * acc_sc[...] + jnp.dot(
        weights.astype(jnp.bfloat16), block, preferred_element_type=jnp.float32
    )
    m_sc[...] = m_new

    @pl.when(step == steps - 1)
    def _():
        out_ref[...] = (acc_sc[...] / l_sc[...]).astype(out_ref.dtype)


def prefix_attention(group, query, cache, peak, denominator, accum, *, prefix_len, scale):
    rows, width = query.shape
    block_q = min(rows, 1024)
    block_k = 1024
    steps = prefix_len // block_k
    grid = (rows // block_q, steps)
    kernel = functools.partial(flash_kernel, scale=scale, steps=steps)
    return pl.pallas_call(
        kernel,
        out_shape=jax.ShapeDtypeStruct((rows, width), jnp.bfloat16),
        grid_spec=pltpu.PrefetchScalarGridSpec(
            num_scalar_prefetch=1,
            grid=grid,
            in_specs=[
                pl.BlockSpec((block_q, width), lambda i, j, g: (i, 0)),
                pl.BlockSpec((block_k, width), lambda i, j, g: (g[0] * steps + j, 0)),
                pl.BlockSpec((block_q, 1), lambda i, j, g: (i, 0)),
                pl.BlockSpec((block_q, 1), lambda i, j, g: (i, 0)),
                pl.BlockSpec((block_q, width), lambda i, j, g: (i, 0)),
            ],
            out_specs=pl.BlockSpec((block_q, width), lambda i, j, g: (i, 0)),
            scratch_shapes=[
                pltpu.VMEM((block_q, 1), jnp.float32),
                pltpu.VMEM((block_q, 1), jnp.float32),
                pltpu.VMEM((block_q, width), jnp.float32),
            ],
        ),
        compiler_params=pltpu.CompilerParams(dimension_semantics=("arbitrary", "arbitrary")),
        cost_estimate=pl.CostEstimate(
            flops=4 * rows * prefix_len * width,
            transcendentals=rows * prefix_len,
            bytes_accessed=prefix_len * width * 2 + rows * width * 8,
        ),
    )(group, query, cache, peak, denominator, accum)


def local(
    hidden_states,
    attn_gain,
    query_weight,
    key_value_weight,
    sink_logits,
    prefix_cache,
    out_weight,
    ffn_gain,
    router_weight,
    gate_up_weight,
    down_weight,
    route_ids,
    prefix_group,
    suffix_lengths,
):
    token_count = hidden_states.shape[0]
    head_size = HEAD
    model_width = D
    local_heads = query_weight.shape[1] // head_size
    local_kv = key_value_weight.shape[1] // (2 * head_size)
    per_kv = local_heads // local_kv
    query_rows = per_kv * token_count
    req_count = lax.axis_size("req")
    req_index = lax.axis_index("req")
    tp_index = lax.axis_index("tp")
    cache_rows = prefix_cache.shape[0]
    prefix_len = cache_rows * req_count // 2
    score_scale = head_size ** (-0.5)
    col_count = hidden_states.shape[1]
    packed = jnp.concatenate([hidden_states.T, router_weight], axis=1)
    gathered = lax.all_gather(packed, "tp", axis=0, tiled=True)
    full_rows = gathered[:, :token_count].T
    router_full = gathered[:, token_count:]
    normed_attn = rms_rows(full_rows, attn_gain)
    positions = (prefix_len + jnp.arange(token_count, dtype=jnp.int32)).astype(jnp.float32)
    queries = jnp.dot(normed_attn, query_weight, preferred_element_type=jnp.float32)
    fresh = jnp.dot(normed_attn, key_value_weight, preferred_element_type=jnp.float32).reshape(
        token_count, local_kv, 2, head_size
    )
    queries = rotate(queries.reshape(token_count, local_heads, head_size), positions).astype(
        jnp.bfloat16
    )
    new_keys = rotate(fresh[:, :, 0], positions).astype(jnp.bfloat16)
    new_values = fresh[:, :, 1].astype(jnp.bfloat16)
    query_heads = (
        queries.reshape(token_count, local_kv, per_kv, head_size)
        .transpose(1, 2, 0, 3)
        .reshape(local_kv, query_rows, head_size)
    )
    assert local_kv == 1
    query_flat = query_heads.reshape(query_rows, head_size)
    fresh_kv = jnp.concatenate([new_keys[:, 0, :], new_values[:, 0, :]], axis=1)
    sink_rows = jnp.broadcast_to(
        sink_logits.reshape(per_kv, 1), (per_kv, token_count)
    ).reshape(query_rows, 1)
    row_pos = jnp.arange(query_rows, dtype=jnp.int32) % token_count
    causal = jnp.arange(token_count, dtype=jnp.int32)[None, :] <= row_pos[:, None]
    fresh_scores = (
        jnp.dot(query_flat, new_keys[:, 0, :].T, preferred_element_type=jnp.float32) * score_scale
    )
    fresh_scores = jnp.where(causal, fresh_scores, -jnp.inf)
    start_peak = jnp.maximum(sink_rows, jnp.max(fresh_scores, axis=1, keepdims=True))
    fresh_weights = jnp.exp(fresh_scores - start_peak)
    start_denominator = jnp.exp(sink_rows - start_peak) + jnp.sum(
        fresh_weights, axis=1, keepdims=True
    )
    start_accum = jnp.dot(
        fresh_weights.astype(jnp.bfloat16), fresh_kv, preferred_element_type=jnp.float32
    )
    query_padded = jnp.concatenate([query_flat, jnp.zeros_like(query_flat)], axis=1)
    own_group = prefix_group[req_index].reshape(1)
    shard_rows = lax.all_gather(prefix_cache, "req", axis=0, tiled=True)
    mixed_wide = prefix_attention(
        own_group, query_padded, shard_rows, start_peak, start_denominator, start_accum,
        prefix_len=prefix_len, scale=score_scale,
    )
    mixed = mixed_wide[:, head_size:].reshape(local_heads, token_count, head_size)
    attn_part = jnp.einsum(
        "hqd,hdo->qo",
        mixed,
        out_weight.reshape(local_heads, head_size, model_width),
        preferred_element_type=jnp.float32,
    )
    attn_full = lax.psum(attn_part, "tp")
    attn_sum = lax.dynamic_slice_in_dim(attn_full, tp_index * col_count, col_count, 1)
    live = (jnp.arange(token_count, dtype=jnp.int32) < suffix_lengths[req_index])[:, None]
    attn_out = jnp.where(live, attn_sum, 0.0).astype(jnp.bfloat16)
    expert_count = router_weight.shape[1]
    top_count = route_ids.shape[1]
    capacity = token_count * top_count * 3 // (2 * expert_count)
    entries = route_ids.reshape(-1)
    onehot = (entries[:, None] == jnp.arange(expert_count, dtype=jnp.int32)[None, :]).astype(
        jnp.int32
    )
    earlier = jnp.cumsum(onehot, axis=0) - onehot
    slots = jnp.sum(earlier * onehot, axis=1)
    targets = entries * capacity + slots
    sources = jnp.arange(token_count * top_count, dtype=jnp.int32) // top_count
    source_of = jnp.zeros((expert_count * capacity,), jnp.int32).at[targets].set(sources)
    filled = jnp.zeros((expert_count * capacity,), jnp.bool_).at[targets].set(True)
    exp_local = gate_up_weight.shape[0]
    ff_local = gate_up_weight.shape[3]
    joined_weight = gate_up_weight.reshape(exp_local, model_width, 2 * ff_local)
    resid_rows = (full_rows.astype(jnp.float32) + attn_full).astype(jnp.bfloat16)
    normed_rows = rms_rows(resid_rows, ffn_gain)
    picked_rows = jnp.where(filled[:, None], normed_rows[source_of], jnp.zeros((), jnp.bfloat16))
    arrived = lax.all_to_all(
        picked_rows.reshape(expert_count, capacity, normed_rows.shape[1]),
        "req",
        split_axis=0,
        concat_axis=0,
        tiled=True,
    )
    item_count = arrived.shape[1]
    grouped = arrived.reshape(req_count, exp_local, item_count, model_width)
    projected = jnp.einsum(
        "sepd,edf->sepf", grouped, joined_weight, preferred_element_type=jnp.float32
    )
    gate_value = jnp.minimum(projected[..., :ff_local], clamp_limit)
    up_value = jnp.clip(projected[..., ff_local:], -clamp_limit, clamp_limit)
    active = ((up_value + 1.0) * gate_value * jax.nn.sigmoid(glu_alpha * gate_value)).astype(
        jnp.bfloat16
    )
    results = jnp.einsum(
        "sepf,efd->sepd", active, down_weight, preferred_element_type=jnp.float32
    ).astype(jnp.bfloat16)
    send_results = results.reshape(arrived.shape[0], item_count, model_width)
    returned = lax.all_to_all(send_results, "req", split_axis=0, concat_axis=0, tiled=True)
    logits = jnp.dot(normed_rows, router_full, preferred_element_type=jnp.float32)
    chosen = jnp.take_along_axis(logits, route_ids, axis=1)
    raised = jnp.exp(chosen)
    gates = raised / jnp.sum(raised, axis=1, keepdims=True)
    picked_back = returned.reshape(expert_count * capacity, model_width)[targets]
    combined = jnp.sum(
        picked_back.reshape(token_count, top_count, model_width).astype(jnp.float32)
        * gates[:, :, None],
        axis=1,
    )
    moe_sum = lax.psum_scatter(combined, "tp", scatter_dimension=1, tiled=True)
    moe_out = jnp.where(live, moe_sum, 0.0).astype(jnp.bfloat16)
    return (attn_out, moe_out)


def solution(mesh):
    return jax.shard_map(
        local,
        mesh=mesh,
        in_specs=(
            P("req", "tp"),
            P(),
            P(None, "tp"),
            P(None, "tp"),
            P("tp"),
            P("req", "tp"),
            P("tp", None),
            P(),
            P("tp", None),
            P("req", None, None, "tp"),
            P("req", "tp", None),
            P("req", None),
            P(),
            P(),
        ),
        out_specs=(P("req", "tp"), P("req", "tp")),
        check_vma=False,
    )
```

```python
import functools

import jax
import jax.numpy as jnp
from jax import lax
from jax.experimental import pallas as pl
from jax.experimental.pallas import tpu as pltpu
from jax.sharding import PartitionSpec as P

D = 2880
HEAD = 64


rope_base = 150000.0
norm_eps = 1e-05
clamp_limit = 7.0
glu_alpha = 1.702


def rms_rows(values, gain):
    wide = values.astype(jnp.float32)
    factor = lax.rsqrt(jnp.mean(wide * wide, axis=1, keepdims=True) + norm_eps)
    return (wide * factor * gain).astype(jnp.bfloat16)


def rotate(values, positions):
    half_size = values.shape[-1] // 2
    powers = jnp.arange(half_size, dtype=jnp.float32) * (-2.0 / values.shape[-1])
    angles = positions[:, None, None] * rope_base**powers
    cosine = jnp.cos(angles)
    sine_part = jnp.sin(angles)
    first_half = values[..., :half_size]
    second_half = values[..., half_size:]
    return jnp.concatenate(
        [
            first_half * cosine - second_half * sine_part,
            second_half * cosine + first_half * sine_part,
        ],
        axis=-1,
    )


def flash_kernel(group_ref, q_ref, kv_ref, m0_ref, l0_ref, acc0_ref, out_ref, m_sc, l_sc, acc_sc, *, scale, steps):
    step = pl.program_id(1)

    @pl.when(step == 0)
    def _():
        m_sc[...] = m0_ref[...]
        l_sc[...] = l0_ref[...]
        acc_sc[...] = acc0_ref[...]

    block = kv_ref[...]
    scores = (
        lax.dot_general(
            q_ref[...], block, (((1,), (1,)), ((), ())), preferred_element_type=jnp.float32
        )
        * scale
    )
    m_prev = m_sc[...]
    m_new = jnp.maximum(m_prev, jnp.max(scores, axis=1, keepdims=True))
    weights = jnp.exp(scores - m_new)
    decay = jnp.exp(m_prev - m_new)
    l_sc[...] = decay * l_sc[...] + jnp.sum(weights, axis=1, keepdims=True)
    acc_sc[...] = decay * acc_sc[...] + jnp.dot(
        weights.astype(jnp.bfloat16), block, preferred_element_type=jnp.float32
    )
    m_sc[...] = m_new

    @pl.when(step == steps - 1)
    def _():
        out_ref[...] = (acc_sc[...] / l_sc[...]).astype(out_ref.dtype)


def prefix_attention(group, query, cache, peak, denominator, accum, *, prefix_len, scale):
    rows, width = query.shape
    block_q = min(rows, 1024)
    block_k = 1024
    steps = prefix_len // block_k
    grid = (rows // block_q, steps)
    kernel = functools.partial(flash_kernel, scale=scale, steps=steps)
    return pl.pallas_call(
        kernel,
        out_shape=jax.ShapeDtypeStruct((rows, width), jnp.bfloat16),
        grid_spec=pltpu.PrefetchScalarGridSpec(
            num_scalar_prefetch=1,
            grid=grid,
            in_specs=[
                pl.BlockSpec((block_q, width), lambda i, j, g: (i, 0)),
                pl.BlockSpec((block_k, width), lambda i, j, g: (g[0] * steps + j, 0)),
                pl.BlockSpec((block_q, 1), lambda i, j, g: (i, 0)),
                pl.BlockSpec((block_q, 1), lambda i, j, g: (i, 0)),
                pl.BlockSpec((block_q, width), lambda i, j, g: (i, 0)),
            ],
            out_specs=pl.BlockSpec((block_q, width), lambda i, j, g: (i, 0)),
            scratch_shapes=[
                pltpu.VMEM((block_q, 1), jnp.float32),
                pltpu.VMEM((block_q, 1), jnp.float32),
                pltpu.VMEM((block_q, width), jnp.float32),
            ],
        ),
        compiler_params=pltpu.CompilerParams(dimension_semantics=("arbitrary", "arbitrary")),
        cost_estimate=pl.CostEstimate(
            flops=4 * rows * prefix_len * width,
            transcendentals=rows * prefix_len,
            bytes_accessed=prefix_len * width * 2 + rows * width * 8,
        ),
    )(group, query, cache, peak, denominator, accum)


def local(
    hidden_states,
    attn_gain,
    query_weight,
    key_value_weight,
    sink_logits,
    prefix_cache,
    out_weight,
    ffn_gain,
    router_weight,
    gate_up_weight,
    down_weight,
    route_ids,
    prefix_group,
    suffix_lengths,
):
    token_count = hidden_states.shape[0]
    head_size = HEAD
    model_width = D
    local_heads = query_weight.shape[1] // head_size
    local_kv = key_value_weight.shape[1] // (2 * head_size)
    per_kv = local_heads // local_kv
    query_rows = per_kv * token_count
    req_count = lax.axis_size("req")
    req_index = lax.axis_index("req")
    tp_index = lax.axis_index("tp")
    cache_rows = prefix_cache.shape[0]
    prefix_len = cache_rows * req_count // 2
    score_scale = head_size ** (-0.5)
    col_count = hidden_states.shape[1]
    packed = jnp.concatenate([hidden_states.T, router_weight], axis=1)
    gathered = lax.all_gather(packed, "tp", axis=0, tiled=True)
    full_rows = gathered[:, :token_count].T
    router_full = gathered[:, token_count:]
    normed_attn = rms_rows(full_rows, attn_gain)
    positions = (prefix_len + jnp.arange(token_count, dtype=jnp.int32)).astype(jnp.float32)
    queries = jnp.dot(normed_attn, query_weight, preferred_element_type=jnp.float32)
    fresh = jnp.dot(normed_attn, key_value_weight, preferred_element_type=jnp.float32).reshape(
        token_count, local_kv, 2, head_size
    )
    queries = rotate(queries.reshape(token_count, local_heads, head_size), positions).astype(
        jnp.bfloat16
    )
    new_keys = rotate(fresh[:, :, 0], positions).astype(jnp.bfloat16)
    new_values = fresh[:, :, 1].astype(jnp.bfloat16)
    query_heads = (
        queries.reshape(token_count, local_kv, per_kv, head_size)
        .transpose(1, 2, 0, 3)
        .reshape(local_kv, query_rows, head_size)
    )
    assert local_kv == 1
    query_flat = query_heads.reshape(query_rows, head_size)
    fresh_kv = jnp.concatenate([new_keys[:, 0, :], new_values[:, 0, :]], axis=1)
    sink_rows = jnp.broadcast_to(
        sink_logits.reshape(per_kv, 1), (per_kv, token_count)
    ).reshape(query_rows, 1)
    row_pos = jnp.arange(query_rows, dtype=jnp.int32) % token_count
    causal = jnp.arange(token_count, dtype=jnp.int32)[None, :] <= row_pos[:, None]
    fresh_scores = (
        jnp.dot(query_flat, new_keys[:, 0, :].T, preferred_element_type=jnp.float32) * score_scale
    )
    fresh_scores = jnp.where(causal, fresh_scores, -jnp.inf)
    start_peak = jnp.maximum(sink_rows, jnp.max(fresh_scores, axis=1, keepdims=True))
    fresh_weights = jnp.exp(fresh_scores - start_peak)
    start_denominator = jnp.exp(sink_rows - start_peak) + jnp.sum(
        fresh_weights, axis=1, keepdims=True
    )
    start_accum = jnp.dot(
        fresh_weights.astype(jnp.bfloat16), fresh_kv, preferred_element_type=jnp.float32
    )
    query_padded = jnp.concatenate([query_flat, jnp.zeros_like(query_flat)], axis=1)
    own_group = prefix_group[req_index].reshape(1)
    shard_rows = lax.all_gather(prefix_cache, "req", axis=0, tiled=True)
    mixed_wide = prefix_attention(
        own_group, query_padded, shard_rows, start_peak, start_denominator, start_accum,
        prefix_len=prefix_len, scale=score_scale,
    )
    mixed = mixed_wide[:, head_size:].reshape(local_heads, token_count, head_size)
    attn_part = jnp.einsum(
        "hqd,hdo->qo",
        mixed,
        out_weight.reshape(local_heads, head_size, model_width),
        preferred_element_type=jnp.float32,
    )
    attn_full = lax.psum(attn_part, "tp")
    attn_sum = lax.dynamic_slice_in_dim(attn_full, tp_index * col_count, col_count, 1)
    live = (jnp.arange(token_count, dtype=jnp.int32) < suffix_lengths[req_index])[:, None]
    attn_out = jnp.where(live, attn_sum, 0.0).astype(jnp.bfloat16)
    expert_count = router_weight.shape[1]
    top_count = route_ids.shape[1]
    capacity = token_count * top_count * 3 // (2 * expert_count)
    entries = route_ids.reshape(-1)
    onehot = (entries[:, None] == jnp.arange(expert_count, dtype=jnp.int32)[None, :]).astype(
        jnp.int32
    )
    earlier = jnp.cumsum(onehot, axis=0) - onehot
    slots = jnp.sum(earlier * onehot, axis=1)
    targets = entries * capacity + slots
    sources = jnp.arange(token_count * top_count, dtype=jnp.int32) // top_count
    source_of = jnp.zeros((expert_count * capacity,), jnp.int32).at[targets].set(sources)
    filled = jnp.zeros((expert_count * capacity,), jnp.bool_).at[targets].set(True)
    exp_local = gate_up_weight.shape[0]
    ff_local = gate_up_weight.shape[3]
    joined_weight = gate_up_weight.reshape(exp_local, model_width, 2 * ff_local)
    resid_rows = (full_rows.astype(jnp.float32) + attn_full).astype(jnp.bfloat16)
    normed_rows = rms_rows(resid_rows, ffn_gain)
    slot_hit = (
        targets.reshape(token_count, top_count)[:, :, None]
        == jnp.arange(expert_count * capacity, dtype=jnp.int32)[None, None, :]
    )
    token_slot = jnp.any(slot_hit, axis=1).astype(jnp.bfloat16)
    picked_rows = lax.dot_general(
        token_slot, normed_rows, (((0,), (0,)), ((), ())), preferred_element_type=jnp.float32
    ).astype(jnp.bfloat16)
    arrived = lax.all_to_all(
        picked_rows.reshape(expert_count, capacity, normed_rows.shape[1]),
        "req",
        split_axis=0,
        concat_axis=0,
        tiled=True,
    )
    item_count = arrived.shape[1]
    grouped = arrived.reshape(req_count, exp_local, item_count, model_width)
    projected = jnp.einsum(
        "sepd,edf->sepf", grouped, joined_weight, preferred_element_type=jnp.float32
    )
    gate_value = jnp.minimum(projected[..., :ff_local], clamp_limit)
    up_value = jnp.clip(projected[..., ff_local:], -clamp_limit, clamp_limit)
    active = ((up_value + 1.0) * gate_value * jax.nn.sigmoid(glu_alpha * gate_value)).astype(
        jnp.bfloat16
    )
    results = jnp.einsum(
        "sepf,efd->sepd", active, down_weight, preferred_element_type=jnp.float32
    ).astype(jnp.bfloat16)
    send_results = results.reshape(arrived.shape[0], item_count, model_width)
    returned = lax.all_to_all(send_results, "req", split_axis=0, concat_axis=0, tiled=True)
    logits = jnp.dot(normed_rows, router_full, preferred_element_type=jnp.float32)
    chosen = jnp.take_along_axis(logits, route_ids, axis=1)
    raised = jnp.exp(chosen)
    gates = raised / jnp.sum(raised, axis=1, keepdims=True)
    gate_slot = jnp.sum(jnp.where(slot_hit, gates[:, :, None], 0.0), axis=1)
    combined = jnp.dot(
        gate_slot,
        returned.reshape(expert_count * capacity, model_width).astype(jnp.float32),
        precision=lax.Precision.HIGHEST,
        preferred_element_type=jnp.float32,
    )
    moe_sum = lax.psum_scatter(combined, "tp", scatter_dimension=1, tiled=True)
    moe_out = jnp.where(live, moe_sum, 0.0).astype(jnp.bfloat16)
    return (attn_out, moe_out)


def solution(mesh):
    return jax.shard_map(
        local,
        mesh=mesh,
        in_specs=(
            P("req", "tp"),
            P(),
            P(None, "tp"),
            P(None, "tp"),
            P("tp"),
            P("req", "tp"),
            P("tp", None),
            P(),
            P("tp", None),
            P("req", None, None, "tp"),
            P("req", "tp", None),
            P("req", None),
            P(),
            P(),
        ),
        out_specs=(P("req", "tp"), P("req", "tp")),
        check_vma=False,
    )
```

```python
import functools

import jax
import jax.numpy as jnp
from jax import lax
from jax.experimental import pallas as pl
from jax.experimental.pallas import tpu as pltpu
from jax.sharding import PartitionSpec as P

D = 2880
HEAD = 64


rope_base = 150000.0
norm_eps = 1e-05
clamp_limit = 7.0
glu_alpha = 1.702


def rms_rows(values, gain):
    wide = values.astype(jnp.float32)
    factor = lax.rsqrt(jnp.mean(wide * wide, axis=1, keepdims=True) + norm_eps)
    return (wide * factor * gain).astype(jnp.bfloat16)


def rotate(values, positions):
    half_size = values.shape[-1] // 2
    powers = jnp.arange(half_size, dtype=jnp.float32) * (-2.0 / values.shape[-1])
    angles = positions[:, None, None] * rope_base**powers
    cosine = jnp.cos(angles)
    sine_part = jnp.sin(angles)
    first_half = values[..., :half_size]
    second_half = values[..., half_size:]
    return jnp.concatenate(
        [
            first_half * cosine - second_half * sine_part,
            second_half * cosine + first_half * sine_part,
        ],
        axis=-1,
    )


def flash_kernel(group_ref, q_ref, kv_ref, m0_ref, l0_ref, acc0_ref, out_ref, m_sc, l_sc, acc_sc, *, scale, steps):
    step = pl.program_id(1)

    @pl.when(step == 0)
    def _():
        m_sc[...] = m0_ref[...]
        l_sc[...] = l0_ref[...]
        acc_sc[...] = acc0_ref[...]

    block = kv_ref[...]
    scores = (
        lax.dot_general(
            q_ref[...], block, (((1,), (1,)), ((), ())), preferred_element_type=jnp.float32
        )
        * scale
    )
    m_prev = m_sc[...]
    m_new = jnp.maximum(m_prev, jnp.max(scores, axis=1, keepdims=True))
    weights = jnp.exp(scores - m_new)
    decay = jnp.exp(m_prev - m_new)
    l_sc[...] = decay * l_sc[...] + jnp.sum(weights, axis=1, keepdims=True)
    acc_sc[...] = decay * acc_sc[...] + jnp.dot(
        weights.astype(jnp.bfloat16), block, preferred_element_type=jnp.float32
    )
    m_sc[...] = m_new

    @pl.when(step == steps - 1)
    def _():
        out_ref[...] = (acc_sc[...] / l_sc[...]).astype(out_ref.dtype)


def prefix_attention(group, query, cache, peak, denominator, accum, *, prefix_len, scale):
    rows, width = query.shape
    block_q = min(rows, 1024)
    block_k = 1024
    steps = prefix_len // block_k
    grid = (rows // block_q, steps)
    kernel = functools.partial(flash_kernel, scale=scale, steps=steps)
    return pl.pallas_call(
        kernel,
        out_shape=jax.ShapeDtypeStruct((rows, width), jnp.bfloat16),
        grid_spec=pltpu.PrefetchScalarGridSpec(
            num_scalar_prefetch=1,
            grid=grid,
            in_specs=[
                pl.BlockSpec((block_q, width), lambda i, j, g: (i, 0)),
                pl.BlockSpec((block_k, width), lambda i, j, g: (g[0] * steps + j, 0)),
                pl.BlockSpec((block_q, 1), lambda i, j, g: (i, 0)),
                pl.BlockSpec((block_q, 1), lambda i, j, g: (i, 0)),
                pl.BlockSpec((block_q, width), lambda i, j, g: (i, 0)),
            ],
            out_specs=pl.BlockSpec((block_q, width), lambda i, j, g: (i, 0)),
            scratch_shapes=[
                pltpu.VMEM((block_q, 1), jnp.float32),
                pltpu.VMEM((block_q, 1), jnp.float32),
                pltpu.VMEM((block_q, width), jnp.float32),
            ],
        ),
        compiler_params=pltpu.CompilerParams(dimension_semantics=("arbitrary", "arbitrary")),
        cost_estimate=pl.CostEstimate(
            flops=4 * rows * prefix_len * width,
            transcendentals=rows * prefix_len,
            bytes_accessed=prefix_len * width * 2 + rows * width * 8,
        ),
    )(group, query, cache, peak, denominator, accum)


def local(
    hidden_states,
    attn_gain,
    query_weight,
    key_value_weight,
    sink_logits,
    prefix_cache,
    out_weight,
    ffn_gain,
    router_weight,
    gate_up_weight,
    down_weight,
    route_ids,
    prefix_group,
    suffix_lengths,
):
    token_count = hidden_states.shape[0]
    head_size = HEAD
    model_width = D
    local_heads = query_weight.shape[1] // head_size
    local_kv = key_value_weight.shape[1] // (2 * head_size)
    per_kv = local_heads // local_kv
    query_rows = per_kv * token_count
    req_count = lax.axis_size("req")
    req_index = lax.axis_index("req")
    tp_index = lax.axis_index("tp")
    cache_rows = prefix_cache.shape[0]
    prefix_len = cache_rows * req_count // 2
    score_scale = head_size ** (-0.5)
    col_count = hidden_states.shape[1]
    packed = jnp.concatenate([hidden_states.T, router_weight], axis=1)
    gathered = lax.all_gather(packed, "tp", axis=0, tiled=True)
    full_rows = gathered[:, :token_count].T
    router_full = gathered[:, token_count:]
    normed_attn = rms_rows(full_rows, attn_gain)
    positions = (prefix_len + jnp.arange(token_count, dtype=jnp.int32)).astype(jnp.float32)
    queries = jnp.dot(normed_attn, query_weight, preferred_element_type=jnp.float32)
    fresh = jnp.dot(normed_attn, key_value_weight, preferred_element_type=jnp.float32).reshape(
        token_count, local_kv, 2, head_size
    )
    queries = rotate(queries.reshape(token_count, local_heads, head_size), positions).astype(
        jnp.bfloat16
    )
    new_keys = rotate(fresh[:, :, 0], positions).astype(jnp.bfloat16)
    new_values = fresh[:, :, 1].astype(jnp.bfloat16)
    query_heads = (
        queries.reshape(token_count, local_kv, per_kv, head_size)
        .transpose(1, 2, 0, 3)
        .reshape(local_kv, query_rows, head_size)
    )
    assert local_kv == 1
    query_flat = query_heads.reshape(query_rows, head_size)
    fresh_kv = jnp.concatenate([new_keys[:, 0, :], new_values[:, 0, :]], axis=1)
    sink_rows = jnp.broadcast_to(
        sink_logits.reshape(per_kv, 1), (per_kv, token_count)
    ).reshape(query_rows, 1)
    row_pos = jnp.arange(query_rows, dtype=jnp.int32) % token_count
    causal = jnp.arange(token_count, dtype=jnp.int32)[None, :] <= row_pos[:, None]
    fresh_scores = (
        jnp.dot(query_flat, new_keys[:, 0, :].T, preferred_element_type=jnp.float32) * score_scale
    )
    fresh_scores = jnp.where(causal, fresh_scores, -jnp.inf)
    start_peak = jnp.maximum(sink_rows, jnp.max(fresh_scores, axis=1, keepdims=True))
    fresh_weights = jnp.exp(fresh_scores - start_peak)
    start_denominator = jnp.exp(sink_rows - start_peak) + jnp.sum(
        fresh_weights, axis=1, keepdims=True
    )
    start_accum = jnp.dot(
        fresh_weights.astype(jnp.bfloat16), fresh_kv, preferred_element_type=jnp.float32
    )
    query_padded = jnp.concatenate([query_flat, jnp.zeros_like(query_flat)], axis=1)
    own_group = prefix_group[req_index].reshape(1)
    shard_rows = lax.all_gather(prefix_cache, "req", axis=0, tiled=True)
    mixed_wide = prefix_attention(
        own_group, query_padded, shard_rows, start_peak, start_denominator, start_accum,
        prefix_len=prefix_len, scale=score_scale,
    )
    mixed = mixed_wide[:, head_size:].reshape(local_heads, token_count, head_size)
    attn_part = jnp.einsum(
        "hqd,hdo->qo",
        mixed,
        out_weight.reshape(local_heads, head_size, model_width),
        preferred_element_type=jnp.float32,
    )
    attn_sum = lax.psum_scatter(attn_part, "tp", scatter_dimension=1, tiled=True)
    live = (jnp.arange(token_count, dtype=jnp.int32) < suffix_lengths[req_index])[:, None]
    attn_out = jnp.where(live, attn_sum, 0.0).astype(jnp.bfloat16)
    expert_count = router_weight.shape[1]
    top_count = route_ids.shape[1]
    capacity = token_count * top_count * 3 // (2 * expert_count)
    entries = route_ids.reshape(-1)
    onehot = (entries[:, None] == jnp.arange(expert_count, dtype=jnp.int32)[None, :]).astype(
        jnp.int32
    )
    earlier = jnp.cumsum(onehot, axis=0) - onehot
    slots = jnp.sum(earlier * onehot, axis=1)
    targets = entries * capacity + slots
    sources = jnp.arange(token_count * top_count, dtype=jnp.int32) // top_count
    source_of = jnp.zeros((expert_count * capacity,), jnp.int32).at[targets].set(sources)
    filled = jnp.zeros((expert_count * capacity,), jnp.bool_).at[targets].set(True)
    exp_local = gate_up_weight.shape[0]
    ff_local = gate_up_weight.shape[3]
    joined_weight = gate_up_weight.reshape(exp_local, model_width, 2 * ff_local)
    resid = (hidden_states.astype(jnp.float32) + attn_sum).astype(jnp.bfloat16)
    resid_rows = lax.all_gather(resid, "tp", axis=1, tiled=True)
    normed_rows = rms_rows(resid_rows, ffn_gain)
    slot_hit = (
        targets.reshape(token_count, top_count)[:, :, None]
        == jnp.arange(expert_count * capacity, dtype=jnp.int32)[None, None, :]
    )
    token_slot = jnp.any(slot_hit, axis=1).astype(jnp.bfloat16)
    picked_rows = lax.dot_general(
        token_slot, normed_rows, (((0,), (0,)), ((), ())), preferred_element_type=jnp.float32
    ).astype(jnp.bfloat16)
    arrived = lax.all_to_all(
        picked_rows.reshape(expert_count, capacity, normed_rows.shape[1]),
        "req",
        split_axis=0,
        concat_axis=0,
        tiled=True,
    )
    item_count = arrived.shape[1]
    grouped = arrived.reshape(req_count, exp_local, item_count, model_width)
    projected = jnp.einsum(
        "sepd,edf->sepf", grouped, joined_weight, preferred_element_type=jnp.float32
    )
    gate_value = jnp.minimum(projected[..., :ff_local], clamp_limit)
    up_value = jnp.clip(projected[..., ff_local:], -clamp_limit, clamp_limit)
    active = ((up_value + 1.0) * gate_value * jax.nn.sigmoid(glu_alpha * gate_value)).astype(
        jnp.bfloat16
    )
    results = jnp.einsum(
        "sepf,efd->sepd", active, down_weight, preferred_element_type=jnp.float32
    ).astype(jnp.bfloat16)
    send_results = results.reshape(arrived.shape[0], item_count, model_width)
    returned = lax.all_to_all(send_results, "req", split_axis=0, concat_axis=0, tiled=True)
    logits = jnp.dot(normed_rows, router_full, preferred_element_type=jnp.float32)
    chosen = jnp.take_along_axis(logits, route_ids, axis=1)
    raised = jnp.exp(chosen)
    gates = raised / jnp.sum(raised, axis=1, keepdims=True)
    gate_slot = jnp.sum(jnp.where(slot_hit, gates[:, :, None], 0.0), axis=1)
    combined = jnp.dot(
        gate_slot,
        returned.reshape(expert_count * capacity, model_width).astype(jnp.float32),
        precision=lax.Precision.HIGHEST,
        preferred_element_type=jnp.float32,
    )
    moe_sum = lax.psum_scatter(combined, "tp", scatter_dimension=1, tiled=True)
    moe_out = jnp.where(live, moe_sum, 0.0).astype(jnp.bfloat16)
    return (attn_out, moe_out)


def solution(mesh):
    return jax.shard_map(
        local,
        mesh=mesh,
        in_specs=(
            P("req", "tp"),
            P(),
            P(None, "tp"),
            P(None, "tp"),
            P("tp"),
            P("req", "tp"),
            P("tp", None),
            P(),
            P("tp", None),
            P("req", None, None, "tp"),
            P("req", "tp", None),
            P("req", None),
            P(),
            P(),
        ),
        out_specs=(P("req", "tp"), P("req", "tp")),
        check_vma=False,
    )
```

```python
import functools

import jax
import jax.numpy as jnp
from jax import lax
from jax.experimental import pallas as pl
from jax.experimental.pallas import tpu as pltpu
from jax.sharding import PartitionSpec as P

D = 2880
HEAD = 64


rope_base = 150000.0
norm_eps = 1e-05
clamp_limit = 7.0
glu_alpha = 1.702


def rms_rows(values, gain):
    wide = values.astype(jnp.float32)
    factor = lax.rsqrt(jnp.mean(wide * wide, axis=1, keepdims=True) + norm_eps)
    return (wide * factor * gain).astype(jnp.bfloat16)


def rotate(values, positions):
    half_size = values.shape[-1] // 2
    powers = jnp.arange(half_size, dtype=jnp.float32) * (-2.0 / values.shape[-1])
    angles = positions[:, None, None] * rope_base**powers
    cosine = jnp.cos(angles)
    sine_part = jnp.sin(angles)
    first_half = values[..., :half_size]
    second_half = values[..., half_size:]
    return jnp.concatenate(
        [
            first_half * cosine - second_half * sine_part,
            second_half * cosine + first_half * sine_part,
        ],
        axis=-1,
    )


def flash_kernel(group_ref, q_ref, kv_ref, m0_ref, l0_ref, acc0_ref, out_ref, m_sc, l_sc, acc_sc, *, scale, steps):
    step = pl.program_id(1)

    @pl.when(step == 0)
    def _():
        m_sc[...] = m0_ref[...]
        l_sc[...] = l0_ref[...]
        acc_sc[...] = acc0_ref[...]

    block = kv_ref[...]
    scores = (
        lax.dot_general(
            q_ref[...], block, (((1,), (1,)), ((), ())), preferred_element_type=jnp.float32
        )
        * scale
    )
    m_prev = m_sc[...]
    m_new = jnp.maximum(m_prev, jnp.max(scores, axis=1, keepdims=True))
    weights = jnp.exp(scores - m_new)
    decay = jnp.exp(m_prev - m_new)
    l_sc[...] = decay * l_sc[...] + jnp.sum(weights, axis=1, keepdims=True)
    acc_sc[...] = decay * acc_sc[...] + jnp.dot(
        weights.astype(jnp.bfloat16), block, preferred_element_type=jnp.float32
    )
    m_sc[...] = m_new

    @pl.when(step == steps - 1)
    def _():
        out_ref[...] = (acc_sc[...] / l_sc[...]).astype(out_ref.dtype)


def prefix_attention(group, query, cache, peak, denominator, accum, *, prefix_len, scale):
    rows, width = query.shape
    block_q = min(rows, 1024)
    block_k = 2048
    steps = prefix_len // block_k
    grid = (rows // block_q, steps)
    kernel = functools.partial(flash_kernel, scale=scale, steps=steps)
    return pl.pallas_call(
        kernel,
        out_shape=jax.ShapeDtypeStruct((rows, width), jnp.bfloat16),
        grid_spec=pltpu.PrefetchScalarGridSpec(
            num_scalar_prefetch=1,
            grid=grid,
            in_specs=[
                pl.BlockSpec((block_q, width), lambda i, j, g: (i, 0)),
                pl.BlockSpec((block_k, width), lambda i, j, g: (g[0] * steps + j, 0)),
                pl.BlockSpec((block_q, 1), lambda i, j, g: (i, 0)),
                pl.BlockSpec((block_q, 1), lambda i, j, g: (i, 0)),
                pl.BlockSpec((block_q, width), lambda i, j, g: (i, 0)),
            ],
            out_specs=pl.BlockSpec((block_q, width), lambda i, j, g: (i, 0)),
            scratch_shapes=[
                pltpu.VMEM((block_q, 1), jnp.float32),
                pltpu.VMEM((block_q, 1), jnp.float32),
                pltpu.VMEM((block_q, width), jnp.float32),
            ],
        ),
        compiler_params=pltpu.CompilerParams(dimension_semantics=("arbitrary", "arbitrary")),
        cost_estimate=pl.CostEstimate(
            flops=4 * rows * prefix_len * width,
            transcendentals=rows * prefix_len,
            bytes_accessed=prefix_len * width * 2 + rows * width * 8,
        ),
    )(group, query, cache, peak, denominator, accum)


def local(
    hidden_states,
    attn_gain,
    query_weight,
    key_value_weight,
    sink_logits,
    prefix_cache,
    out_weight,
    ffn_gain,
    router_weight,
    gate_up_weight,
    down_weight,
    route_ids,
    prefix_group,
    suffix_lengths,
):
    token_count = hidden_states.shape[0]
    head_size = HEAD
    model_width = D
    local_heads = query_weight.shape[1] // head_size
    local_kv = key_value_weight.shape[1] // (2 * head_size)
    per_kv = local_heads // local_kv
    query_rows = per_kv * token_count
    req_count = lax.axis_size("req")
    req_index = lax.axis_index("req")
    tp_index = lax.axis_index("tp")
    cache_rows = prefix_cache.shape[0]
    prefix_len = cache_rows * req_count // 2
    score_scale = head_size ** (-0.5)
    col_count = hidden_states.shape[1]
    packed = jnp.concatenate([hidden_states.T, router_weight], axis=1)
    gathered = lax.all_gather(packed, "tp", axis=0, tiled=True)
    full_rows = gathered[:, :token_count].T
    router_full = gathered[:, token_count:]
    normed_attn = rms_rows(full_rows, attn_gain)
    positions = (prefix_len + jnp.arange(token_count, dtype=jnp.int32)).astype(jnp.float32)
    queries = jnp.dot(normed_attn, query_weight, preferred_element_type=jnp.float32)
    fresh = jnp.dot(normed_attn, key_value_weight, preferred_element_type=jnp.float32).reshape(
        token_count, local_kv, 2, head_size
    )
    queries = rotate(queries.reshape(token_count, local_heads, head_size), positions).astype(
        jnp.bfloat16
    )
    new_keys = rotate(fresh[:, :, 0], positions).astype(jnp.bfloat16)
    new_values = fresh[:, :, 1].astype(jnp.bfloat16)
    query_heads = (
        queries.reshape(token_count, local_kv, per_kv, head_size)
        .transpose(1, 2, 0, 3)
        .reshape(local_kv, query_rows, head_size)
    )
    assert local_kv == 1
    query_flat = query_heads.reshape(query_rows, head_size)
    fresh_kv = jnp.concatenate([new_keys[:, 0, :], new_values[:, 0, :]], axis=1)
    sink_rows = jnp.broadcast_to(
        sink_logits.reshape(per_kv, 1), (per_kv, token_count)
    ).reshape(query_rows, 1)
    row_pos = jnp.arange(query_rows, dtype=jnp.int32) % token_count
    causal = jnp.arange(token_count, dtype=jnp.int32)[None, :] <= row_pos[:, None]
    fresh_scores = (
        jnp.dot(query_flat, new_keys[:, 0, :].T, preferred_element_type=jnp.float32) * score_scale
    )
    fresh_scores = jnp.where(causal, fresh_scores, -jnp.inf)
    start_peak = jnp.maximum(sink_rows, jnp.max(fresh_scores, axis=1, keepdims=True))
    fresh_weights = jnp.exp(fresh_scores - start_peak)
    start_denominator = jnp.exp(sink_rows - start_peak) + jnp.sum(
        fresh_weights, axis=1, keepdims=True
    )
    start_accum = jnp.dot(
        fresh_weights.astype(jnp.bfloat16), fresh_kv, preferred_element_type=jnp.float32
    )
    query_padded = jnp.concatenate([query_flat, jnp.zeros_like(query_flat)], axis=1)
    own_group = prefix_group[req_index].reshape(1)
    shard_rows = lax.all_gather(prefix_cache, "req", axis=0, tiled=True)
    mixed_wide = prefix_attention(
        own_group, query_padded, shard_rows, start_peak, start_denominator, start_accum,
        prefix_len=prefix_len, scale=score_scale,
    )
    mixed = mixed_wide[:, head_size:].reshape(local_heads, token_count, head_size)
    attn_part = jnp.einsum(
        "hqd,hdo->qo",
        mixed,
        out_weight.reshape(local_heads, head_size, model_width),
        preferred_element_type=jnp.float32,
    )
    attn_sum = lax.psum_scatter(attn_part, "tp", scatter_dimension=1, tiled=True)
    live = (jnp.arange(token_count, dtype=jnp.int32) < suffix_lengths[req_index])[:, None]
    attn_out = jnp.where(live, attn_sum, 0.0).astype(jnp.bfloat16)
    expert_count = router_weight.shape[1]
    top_count = route_ids.shape[1]
    capacity = token_count * top_count * 3 // (2 * expert_count)
    entries = route_ids.reshape(-1)
    onehot = (entries[:, None] == jnp.arange(expert_count, dtype=jnp.int32)[None, :]).astype(
        jnp.int32
    )
    earlier = jnp.cumsum(onehot, axis=0) - onehot
    slots = jnp.sum(earlier * onehot, axis=1)
    targets = entries * capacity + slots
    sources = jnp.arange(token_count * top_count, dtype=jnp.int32) // top_count
    source_of = jnp.zeros((expert_count * capacity,), jnp.int32).at[targets].set(sources)
    filled = jnp.zeros((expert_count * capacity,), jnp.bool_).at[targets].set(True)
    exp_local = gate_up_weight.shape[0]
    ff_local = gate_up_weight.shape[3]
    joined_weight = gate_up_weight.reshape(exp_local, model_width, 2 * ff_local)
    resid = (hidden_states.astype(jnp.float32) + attn_sum).astype(jnp.bfloat16)
    resid_rows = lax.all_gather(resid, "tp", axis=1, tiled=True)
    normed_rows = rms_rows(resid_rows, ffn_gain)
    slot_hit = (
        targets.reshape(token_count, top_count)[:, :, None]
        == jnp.arange(expert_count * capacity, dtype=jnp.int32)[None, None, :]
    )
    token_slot = jnp.any(slot_hit, axis=1).astype(jnp.bfloat16)
    picked_rows = lax.dot_general(
        token_slot, normed_rows, (((0,), (0,)), ((), ())), preferred_element_type=jnp.float32
    ).astype(jnp.bfloat16)
    arrived = lax.all_to_all(
        picked_rows.reshape(expert_count, capacity, normed_rows.shape[1]),
        "req",
        split_axis=0,
        concat_axis=0,
        tiled=True,
    )
    item_count = arrived.shape[1]
    grouped = arrived.reshape(req_count, exp_local, item_count, model_width)
    projected = jnp.einsum(
        "sepd,edf->sepf", grouped, joined_weight, preferred_element_type=jnp.float32
    )
    gate_value = jnp.minimum(projected[..., :ff_local], clamp_limit)
    up_value = jnp.clip(projected[..., ff_local:], -clamp_limit, clamp_limit)
    active = ((up_value + 1.0) * gate_value * jax.nn.sigmoid(glu_alpha * gate_value)).astype(
        jnp.bfloat16
    )
    results = jnp.einsum(
        "sepf,efd->sepd", active, down_weight, preferred_element_type=jnp.float32
    ).astype(jnp.bfloat16)
    send_results = results.reshape(arrived.shape[0], item_count, model_width)
    returned = lax.all_to_all(send_results, "req", split_axis=0, concat_axis=0, tiled=True)
    logits = jnp.dot(normed_rows, router_full, preferred_element_type=jnp.float32)
    chosen = jnp.take_along_axis(logits, route_ids, axis=1)
    raised = jnp.exp(chosen)
    gates = raised / jnp.sum(raised, axis=1, keepdims=True)
    gate_slot = jnp.sum(jnp.where(slot_hit, gates[:, :, None], 0.0), axis=1)
    combined = jnp.dot(
        gate_slot,
        returned.reshape(expert_count * capacity, model_width).astype(jnp.float32),
        precision=lax.Precision.HIGHEST,
        preferred_element_type=jnp.float32,
    )
    moe_sum = lax.psum_scatter(combined, "tp", scatter_dimension=1, tiled=True)
    moe_out = jnp.where(live, moe_sum, 0.0).astype(jnp.bfloat16)
    return (attn_out, moe_out)


def solution(mesh):
    return jax.shard_map(
        local,
        mesh=mesh,
        in_specs=(
            P("req", "tp"),
            P(),
            P(None, "tp"),
            P(None, "tp"),
            P("tp"),
            P("req", "tp"),
            P("tp", None),
            P(),
            P("tp", None),
            P("req", None, None, "tp"),
            P("req", "tp", None),
            P("req", None),
            P(),
            P(),
        ),
        out_specs=(P("req", "tp"), P("req", "tp")),
        check_vma=False,
    )
```

```python
import functools

import jax
import jax.numpy as jnp
from jax import lax
from jax.experimental import pallas as pl
from jax.experimental.pallas import tpu as pltpu
from jax.sharding import PartitionSpec as P

D = 2880
HEAD = 64


rope_base = 150000.0
norm_eps = 1e-05
clamp_limit = 7.0
glu_alpha = 1.702


def rms_rows(values, gain):
    wide = values.astype(jnp.float32)
    factor = lax.rsqrt(jnp.mean(wide * wide, axis=1, keepdims=True) + norm_eps)
    return (wide * factor * gain).astype(jnp.bfloat16)


def rotate(values, positions):
    half_size = values.shape[-1] // 2
    powers = jnp.arange(half_size, dtype=jnp.float32) * (-2.0 / values.shape[-1])
    angles = positions[:, None, None] * rope_base**powers
    cosine = jnp.cos(angles)
    sine_part = jnp.sin(angles)
    first_half = values[..., :half_size]
    second_half = values[..., half_size:]
    return jnp.concatenate(
        [
            first_half * cosine - second_half * sine_part,
            second_half * cosine + first_half * sine_part,
        ],
        axis=-1,
    )


def flash_kernel(group_ref, q_ref, kv_ref, m0_ref, l0_ref, acc0_ref, out_ref, m_sc, l_sc, acc_sc, *, scale, steps):
    step = pl.program_id(1)

    @pl.when(step == 0)
    def _():
        m_sc[...] = m0_ref[...]
        l_sc[...] = l0_ref[...]
        acc_sc[...] = acc0_ref[...]

    block = kv_ref[...]
    scores = (
        lax.dot_general(
            q_ref[...], block, (((1,), (1,)), ((), ())), preferred_element_type=jnp.float32
        )
        * scale
    )
    m_prev = m_sc[...]
    m_new = jnp.maximum(m_prev, jnp.max(scores, axis=1, keepdims=True))
    weights = jnp.exp(scores - m_new)
    decay = jnp.exp(m_prev - m_new)
    l_sc[...] = decay * l_sc[...] + jnp.sum(weights, axis=1, keepdims=True)
    acc_sc[...] = decay * acc_sc[...] + jnp.dot(
        weights.astype(jnp.bfloat16), block, preferred_element_type=jnp.float32
    )
    m_sc[...] = m_new

    @pl.when(step == steps - 1)
    def _():
        out_ref[...] = (acc_sc[...] / l_sc[...]).astype(out_ref.dtype)


def prefix_attention(group, query, cache, peak, denominator, accum, *, prefix_len, scale):
    rows, width = query.shape
    block_q = min(rows, 1024)
    block_k = 2048
    steps = prefix_len // block_k
    grid = (rows // block_q, steps)
    kernel = functools.partial(flash_kernel, scale=scale, steps=steps)
    return pl.pallas_call(
        kernel,
        out_shape=jax.ShapeDtypeStruct((rows, width), jnp.bfloat16),
        grid_spec=pltpu.PrefetchScalarGridSpec(
            num_scalar_prefetch=1,
            grid=grid,
            in_specs=[
                pl.BlockSpec((block_q, width), lambda i, j, g: (i, 0)),
                pl.BlockSpec((block_k, width), lambda i, j, g: (g[0] * steps + j, 0)),
                pl.BlockSpec((block_q, 1), lambda i, j, g: (i, 0)),
                pl.BlockSpec((block_q, 1), lambda i, j, g: (i, 0)),
                pl.BlockSpec((block_q, width), lambda i, j, g: (i, 0)),
            ],
            out_specs=pl.BlockSpec((block_q, width), lambda i, j, g: (i, 0)),
            scratch_shapes=[
                pltpu.VMEM((block_q, 1), jnp.float32),
                pltpu.VMEM((block_q, 1), jnp.float32),
                pltpu.VMEM((block_q, width), jnp.float32),
            ],
        ),
        compiler_params=pltpu.CompilerParams(dimension_semantics=("arbitrary", "arbitrary")),
        cost_estimate=pl.CostEstimate(
            flops=4 * rows * prefix_len * width,
            transcendentals=rows * prefix_len,
            bytes_accessed=prefix_len * width * 2 + rows * width * 8,
        ),
    )(group, query, cache, peak, denominator, accum)


def local(
    hidden_states,
    attn_gain,
    query_weight,
    key_value_weight,
    sink_logits,
    prefix_cache,
    out_weight,
    ffn_gain,
    router_weight,
    gate_up_weight,
    down_weight,
    route_ids,
    prefix_group,
    suffix_lengths,
):
    token_count = hidden_states.shape[0]
    head_size = HEAD
    model_width = D
    local_heads = query_weight.shape[1] // head_size
    local_kv = key_value_weight.shape[1] // (2 * head_size)
    per_kv = local_heads // local_kv
    query_rows = per_kv * token_count
    req_count = lax.axis_size("req")
    req_index = lax.axis_index("req")
    tp_index = lax.axis_index("tp")
    cache_rows = prefix_cache.shape[0]
    prefix_len = cache_rows * req_count // 2
    score_scale = head_size ** (-0.5)
    col_count = hidden_states.shape[1]
    packed = jnp.concatenate([hidden_states.T, router_weight], axis=1)
    gathered = lax.all_gather(packed, "tp", axis=0, tiled=True)
    full_rows = gathered[:, :token_count].T
    router_full = gathered[:, token_count:]
    normed_attn = rms_rows(full_rows, attn_gain)
    positions = (prefix_len + jnp.arange(token_count, dtype=jnp.int32)).astype(jnp.float32)
    queries = jnp.dot(normed_attn, query_weight, preferred_element_type=jnp.float32)
    fresh = jnp.dot(normed_attn, key_value_weight, preferred_element_type=jnp.float32).reshape(
        token_count, local_kv, 2, head_size
    )
    queries = rotate(queries.reshape(token_count, local_heads, head_size), positions).astype(
        jnp.bfloat16
    )
    new_keys = rotate(fresh[:, :, 0], positions).astype(jnp.bfloat16)
    new_values = fresh[:, :, 1].astype(jnp.bfloat16)
    query_heads = (
        queries.reshape(token_count, local_kv, per_kv, head_size)
        .transpose(1, 2, 0, 3)
        .reshape(local_kv, query_rows, head_size)
    )
    assert local_kv == 1
    query_flat = query_heads.reshape(query_rows, head_size)
    fresh_kv = jnp.concatenate([new_keys[:, 0, :], new_values[:, 0, :]], axis=1)
    sink_rows = jnp.broadcast_to(
        sink_logits.reshape(per_kv, 1), (per_kv, token_count)
    ).reshape(query_rows, 1)
    row_pos = jnp.arange(query_rows, dtype=jnp.int32) % token_count
    causal = jnp.arange(token_count, dtype=jnp.int32)[None, :] <= row_pos[:, None]
    fresh_scores = (
        jnp.dot(query_flat, new_keys[:, 0, :].T, preferred_element_type=jnp.float32) * score_scale
    )
    fresh_scores = jnp.where(causal, fresh_scores, -jnp.inf)
    start_peak = jnp.maximum(sink_rows, jnp.max(fresh_scores, axis=1, keepdims=True))
    fresh_weights = jnp.exp(fresh_scores - start_peak)
    start_denominator = jnp.exp(sink_rows - start_peak) + jnp.sum(
        fresh_weights, axis=1, keepdims=True
    )
    start_accum = jnp.dot(
        fresh_weights.astype(jnp.bfloat16), fresh_kv, preferred_element_type=jnp.float32
    )
    query_padded = jnp.concatenate([query_flat, jnp.zeros_like(query_flat)], axis=1)
    own_group = prefix_group[req_index].reshape(1)
    shard_rows = lax.all_gather(prefix_cache, "req", axis=0, tiled=True)
    mixed_wide = prefix_attention(
        own_group, query_padded, shard_rows, start_peak, start_denominator, start_accum,
        prefix_len=prefix_len, scale=score_scale,
    )
    mixed = mixed_wide[:, head_size:].reshape(local_heads, token_count, head_size)
    attn_part = jnp.einsum(
        "hqd,hdo->qo",
        mixed,
        out_weight.reshape(local_heads, head_size, model_width),
        preferred_element_type=jnp.float32,
    )
    attn_sum = lax.psum_scatter(attn_part, "tp", scatter_dimension=1, tiled=True)
    live = (jnp.arange(token_count, dtype=jnp.int32) < suffix_lengths[req_index])[:, None]
    attn_out = jnp.where(live, attn_sum, 0.0).astype(jnp.bfloat16)
    expert_count = router_weight.shape[1]
    top_count = route_ids.shape[1]
    capacity = token_count * top_count * 3 // (2 * expert_count)
    entries = route_ids.reshape(-1)
    onehot = (entries[:, None] == jnp.arange(expert_count, dtype=jnp.int32)[None, :]).astype(
        jnp.int32
    )
    earlier = jnp.cumsum(onehot, axis=0) - onehot
    slots = jnp.sum(earlier * onehot, axis=1)
    targets = entries * capacity + slots
    sources = jnp.arange(token_count * top_count, dtype=jnp.int32) // top_count
    source_of = jnp.zeros((expert_count * capacity,), jnp.int32).at[targets].set(sources)
    filled = jnp.zeros((expert_count * capacity,), jnp.bool_).at[targets].set(True)
    exp_local = gate_up_weight.shape[0]
    ff_local = gate_up_weight.shape[3]
    joined_weight = gate_up_weight.reshape(exp_local, model_width, 2 * ff_local)
    resid = (hidden_states.astype(jnp.float32) + attn_sum).astype(jnp.bfloat16)
    resid_rows = lax.all_gather(resid, "tp", axis=1, tiled=True)
    normed_rows = rms_rows(resid_rows, ffn_gain)
    slot_hit = (
        targets.reshape(token_count, top_count)[:, :, None]
        == jnp.arange(expert_count * capacity, dtype=jnp.int32)[None, None, :]
    )
    token_slot = jnp.any(slot_hit, axis=1).astype(jnp.bfloat16)
    picked_rows = lax.dot_general(
        token_slot, normed_rows, (((0,), (0,)), ((), ())), preferred_element_type=jnp.float32
    ).astype(jnp.bfloat16)
    arrived = lax.all_to_all(
        picked_rows.reshape(expert_count, capacity, normed_rows.shape[1]),
        "req",
        split_axis=0,
        concat_axis=0,
        tiled=True,
    )
    item_count = arrived.shape[1]
    grouped = arrived.reshape(req_count, exp_local, item_count, model_width)
    projected = jnp.einsum(
        "sepd,edf->sepf", grouped, joined_weight, preferred_element_type=jnp.float32
    )
    gate_value = jnp.minimum(projected[..., :ff_local], clamp_limit)
    up_value = jnp.clip(projected[..., ff_local:], -clamp_limit, clamp_limit)
    active = ((up_value + 1.0) * gate_value * jax.nn.sigmoid(glu_alpha * gate_value)).astype(
        jnp.bfloat16
    )
    results = jnp.einsum(
        "sepf,efd->sepd", active, down_weight, preferred_element_type=jnp.float32
    ).astype(jnp.bfloat16)
    tp_count = lax.axis_size("tp")
    feat_part = model_width // tp_count
    send_results = (
        results.reshape(req_count, item_count, tp_count, feat_part)
        .transpose(0, 2, 1, 3)
        .reshape(req_count * tp_count, item_count, feat_part)
    )
    returned = lax.all_to_all(
        send_results, ("req", "tp"), split_axis=0, concat_axis=0, tiled=True
    )
    expert_parts = jnp.sum(
        returned.reshape(req_count * exp_local, tp_count, item_count, feat_part).astype(
            jnp.float32
        ),
        axis=1,
    )
    logits = jnp.dot(normed_rows, router_full, preferred_element_type=jnp.float32)
    chosen = jnp.take_along_axis(logits, route_ids, axis=1)
    raised = jnp.exp(chosen)
    gates = raised / jnp.sum(raised, axis=1, keepdims=True)
    gate_slot = jnp.sum(jnp.where(slot_hit, gates[:, :, None], 0.0), axis=1)
    moe_sum = jnp.dot(
        gate_slot,
        expert_parts.reshape(expert_count * capacity, feat_part),
        precision=lax.Precision.HIGHEST,
        preferred_element_type=jnp.float32,
    )
    moe_out = jnp.where(live, moe_sum, 0.0).astype(jnp.bfloat16)
    return (attn_out, moe_out)


def solution(mesh):
    return jax.shard_map(
        local,
        mesh=mesh,
        in_specs=(
            P("req", "tp"),
            P(),
            P(None, "tp"),
            P(None, "tp"),
            P("tp"),
            P("req", "tp"),
            P("tp", None),
            P(),
            P("tp", None),
            P("req", None, None, "tp"),
            P("req", "tp", None),
            P("req", None),
            P(),
            P(),
        ),
        out_specs=(P("req", "tp"), P("req", "tp")),
        check_vma=False,
    )
```

```python
import functools

import jax
import jax.numpy as jnp
from jax import lax
from jax.experimental import pallas as pl
from jax.experimental.pallas import tpu as pltpu
from jax.sharding import PartitionSpec as P

D = 2880
HEAD = 64


rope_base = 150000.0
norm_eps = 1e-05
clamp_limit = 7.0
glu_alpha = 1.702


def rms_rows(values, gain):
    wide = values.astype(jnp.float32)
    factor = lax.rsqrt(jnp.mean(wide * wide, axis=1, keepdims=True) + norm_eps)
    return (wide * factor * gain).astype(jnp.bfloat16)


def rotate(values, positions):
    half_size = values.shape[-1] // 2
    powers = jnp.arange(half_size, dtype=jnp.float32) * (-2.0 / values.shape[-1])
    angles = positions[:, None, None] * rope_base**powers
    cosine = jnp.cos(angles)
    sine_part = jnp.sin(angles)
    first_half = values[..., :half_size]
    second_half = values[..., half_size:]
    return jnp.concatenate(
        [
            first_half * cosine - second_half * sine_part,
            second_half * cosine + first_half * sine_part,
        ],
        axis=-1,
    )


def flash_kernel(group_ref, q_ref, kv_ref, m0_ref, l0_ref, acc0_ref, out_ref, m_sc, l_sc, acc_sc, *, scale, steps):
    step = pl.program_id(1)

    @pl.when(step == 0)
    def _():
        m_sc[...] = m0_ref[...]
        l_sc[...] = l0_ref[...]
        acc_sc[...] = acc0_ref[...]

    block = kv_ref[...]
    scores = (
        lax.dot_general(
            q_ref[...], block, (((1,), (1,)), ((), ())), preferred_element_type=jnp.float32
        )
        * scale
    )
    m_prev = m_sc[...]
    m_new = jnp.maximum(m_prev, jnp.max(scores, axis=1, keepdims=True))
    weights = jnp.exp(scores - m_new)
    decay = jnp.exp(m_prev - m_new)
    l_sc[...] = decay * l_sc[...] + jnp.sum(weights, axis=1, keepdims=True)
    acc_sc[...] = decay * acc_sc[...] + jnp.dot(
        weights.astype(jnp.bfloat16), block, preferred_element_type=jnp.float32
    )
    m_sc[...] = m_new

    @pl.when(step == steps - 1)
    def _():
        out_ref[...] = (acc_sc[...] / l_sc[...]).astype(out_ref.dtype)


def prefix_attention(group, query, cache, peak, denominator, accum, *, prefix_len, scale):
    rows, width = query.shape
    block_q = min(rows, 1024)
    block_k = 2048
    steps = prefix_len // block_k
    grid = (rows // block_q, steps)
    kernel = functools.partial(flash_kernel, scale=scale, steps=steps)
    return pl.pallas_call(
        kernel,
        out_shape=jax.ShapeDtypeStruct((rows, width), jnp.bfloat16),
        grid_spec=pltpu.PrefetchScalarGridSpec(
            num_scalar_prefetch=1,
            grid=grid,
            in_specs=[
                pl.BlockSpec((block_q, width), lambda i, j, g: (i, 0)),
                pl.BlockSpec((block_k, width), lambda i, j, g: (g[0] * steps + j, 0)),
                pl.BlockSpec((block_q, 1), lambda i, j, g: (i, 0)),
                pl.BlockSpec((block_q, 1), lambda i, j, g: (i, 0)),
                pl.BlockSpec((block_q, width), lambda i, j, g: (i, 0)),
            ],
            out_specs=pl.BlockSpec((block_q, width), lambda i, j, g: (i, 0)),
            scratch_shapes=[
                pltpu.VMEM((block_q, 1), jnp.float32),
                pltpu.VMEM((block_q, 1), jnp.float32),
                pltpu.VMEM((block_q, width), jnp.float32),
            ],
        ),
        compiler_params=pltpu.CompilerParams(dimension_semantics=("arbitrary", "arbitrary")),
        cost_estimate=pl.CostEstimate(
            flops=4 * rows * prefix_len * width,
            transcendentals=rows * prefix_len,
            bytes_accessed=prefix_len * width * 2 + rows * width * 8,
        ),
    )(group, query, cache, peak, denominator, accum)


def local(
    hidden_states,
    attn_gain,
    query_weight,
    key_value_weight,
    sink_logits,
    prefix_cache,
    out_weight,
    ffn_gain,
    router_weight,
    gate_up_weight,
    down_weight,
    route_ids,
    prefix_group,
    suffix_lengths,
):
    token_count = hidden_states.shape[0]
    head_size = HEAD
    model_width = D
    local_heads = query_weight.shape[1] // head_size
    local_kv = key_value_weight.shape[1] // (2 * head_size)
    per_kv = local_heads // local_kv
    query_rows = per_kv * token_count
    req_count = lax.axis_size("req")
    req_index = lax.axis_index("req")
    tp_index = lax.axis_index("tp")
    cache_rows = prefix_cache.shape[0]
    prefix_len = cache_rows * req_count // 2
    score_scale = head_size ** (-0.5)
    col_count = hidden_states.shape[1]
    packed = jnp.concatenate([hidden_states.T, router_weight], axis=1)
    gathered = lax.all_gather(packed, "tp", axis=0, tiled=True)
    full_rows = gathered[:, :token_count].T
    router_full = gathered[:, token_count:]
    normed_attn = rms_rows(full_rows, attn_gain)
    positions = (prefix_len + jnp.arange(token_count, dtype=jnp.int32)).astype(jnp.float32)
    queries = jnp.dot(normed_attn, query_weight, preferred_element_type=jnp.float32)
    fresh = jnp.dot(normed_attn, key_value_weight, preferred_element_type=jnp.float32).reshape(
        token_count, local_kv, 2, head_size
    )
    queries = rotate(queries.reshape(token_count, local_heads, head_size), positions).astype(
        jnp.bfloat16
    )
    new_keys = rotate(fresh[:, :, 0], positions).astype(jnp.bfloat16)
    new_values = fresh[:, :, 1].astype(jnp.bfloat16)
    query_heads = (
        queries.reshape(token_count, local_kv, per_kv, head_size)
        .transpose(1, 2, 0, 3)
        .reshape(local_kv, query_rows, head_size)
    )
    assert local_kv == 1
    query_flat = query_heads.reshape(query_rows, head_size)
    fresh_kv = jnp.concatenate([new_keys[:, 0, :], new_values[:, 0, :]], axis=1)
    sink_rows = jnp.broadcast_to(
        sink_logits.reshape(per_kv, 1), (per_kv, token_count)
    ).reshape(query_rows, 1)
    row_pos = jnp.arange(query_rows, dtype=jnp.int32) % token_count
    causal = jnp.arange(token_count, dtype=jnp.int32)[None, :] <= row_pos[:, None]
    fresh_scores = (
        jnp.dot(query_flat, new_keys[:, 0, :].T, preferred_element_type=jnp.float32) * score_scale
    )
    fresh_scores = jnp.where(causal, fresh_scores, -jnp.inf)
    start_peak = jnp.maximum(sink_rows, jnp.max(fresh_scores, axis=1, keepdims=True))
    fresh_weights = jnp.exp(fresh_scores - start_peak)
    start_denominator = jnp.exp(sink_rows - start_peak) + jnp.sum(
        fresh_weights, axis=1, keepdims=True
    )
    start_accum = jnp.dot(
        fresh_weights.astype(jnp.bfloat16), fresh_kv, preferred_element_type=jnp.float32
    )
    query_padded = jnp.concatenate([query_flat, jnp.zeros_like(query_flat)], axis=1)
    own_group = prefix_group[req_index].reshape(1)
    shard_rows = lax.all_gather(prefix_cache, "req", axis=0, tiled=True)
    mixed_wide = prefix_attention(
        own_group, query_padded, shard_rows, start_peak, start_denominator, start_accum,
        prefix_len=prefix_len, scale=score_scale,
    )
    mixed = mixed_wide[:, head_size:].reshape(local_heads, token_count, head_size)
    attn_part = jnp.einsum(
        "hqd,hdo->qo",
        mixed,
        out_weight.reshape(local_heads, head_size, model_width),
        preferred_element_type=jnp.float32,
    )
    attn_sum = lax.psum_scatter(attn_part, "tp", scatter_dimension=1, tiled=True)
    live = (jnp.arange(token_count, dtype=jnp.int32) < suffix_lengths[req_index])[:, None]
    attn_out = jnp.where(live, attn_sum, 0.0).astype(jnp.bfloat16)
    expert_count = router_weight.shape[1]
    top_count = route_ids.shape[1]
    capacity = token_count * top_count * 3 // (2 * expert_count)
    entries = route_ids.reshape(-1)
    onehot = (entries[:, None] == jnp.arange(expert_count, dtype=jnp.int32)[None, :]).astype(
        jnp.int32
    )
    earlier = jnp.cumsum(onehot, axis=0) - onehot
    slots = jnp.sum(earlier * onehot, axis=1)
    targets = entries * capacity + slots
    sources = jnp.arange(token_count * top_count, dtype=jnp.int32) // top_count
    source_of = jnp.zeros((expert_count * capacity,), jnp.int32).at[targets].set(sources)
    filled = jnp.zeros((expert_count * capacity,), jnp.bool_).at[targets].set(True)
    exp_local = gate_up_weight.shape[0]
    ff_local = gate_up_weight.shape[3]
    joined_weight = gate_up_weight.reshape(exp_local, model_width, 2 * ff_local)
    resid = (hidden_states.astype(jnp.float32) + attn_sum).astype(jnp.bfloat16)
    resid_rows = lax.all_gather(resid, "tp", axis=1, tiled=True)
    normed_rows = rms_rows(resid_rows, ffn_gain)
    slot_hit = (
        targets.reshape(token_count, top_count)[:, :, None]
        == jnp.arange(expert_count * capacity, dtype=jnp.int32)[None, None, :]
    )
    token_slot = jnp.any(slot_hit, axis=1).astype(jnp.bfloat16)
    picked_rows = lax.dot_general(
        token_slot, normed_rows, (((0,), (0,)), ((), ())), preferred_element_type=jnp.float32
    ).astype(jnp.bfloat16)
    arrived = lax.all_to_all(
        picked_rows.reshape(expert_count, capacity, normed_rows.shape[1]),
        "req",
        split_axis=0,
        concat_axis=0,
        tiled=True,
    )
    item_count = arrived.shape[1]
    grouped = arrived.reshape(req_count, exp_local, item_count, model_width)
    projected = jnp.einsum(
        "sepd,edf->sepf", grouped, joined_weight, preferred_element_type=jnp.float32
    )
    gate_value = jnp.minimum(projected[..., :ff_local], clamp_limit)
    up_value = jnp.clip(projected[..., ff_local:], -clamp_limit, clamp_limit)
    active = ((up_value + 1.0) * gate_value * jax.nn.sigmoid(glu_alpha * gate_value)).astype(
        jnp.bfloat16
    )
    tp_count = lax.axis_size("tp")
    feat_part = model_width // tp_count
    send_results = jnp.einsum(
        "sepf,eftd->setpd",
        active,
        down_weight.reshape(exp_local, ff_local, tp_count, feat_part),
        preferred_element_type=jnp.float32,
    ).astype(jnp.bfloat16).reshape(req_count * exp_local * tp_count, item_count, feat_part)
    returned = lax.all_to_all(
        send_results, ("req", "tp"), split_axis=0, concat_axis=0, tiled=True
    )
    expert_parts = jnp.sum(
        returned.reshape(req_count * exp_local, tp_count, item_count, feat_part).astype(
            jnp.float32
        ),
        axis=1,
    )
    logits = jnp.dot(normed_rows, router_full, preferred_element_type=jnp.float32)
    chosen = jnp.take_along_axis(logits, route_ids, axis=1)
    raised = jnp.exp(chosen)
    gates = raised / jnp.sum(raised, axis=1, keepdims=True)
    gate_slot = jnp.sum(jnp.where(slot_hit, gates[:, :, None], 0.0), axis=1)
    moe_sum = jnp.dot(
        gate_slot,
        expert_parts.reshape(expert_count * capacity, feat_part),
        precision=lax.Precision.HIGHEST,
        preferred_element_type=jnp.float32,
    )
    moe_out = jnp.where(live, moe_sum, 0.0).astype(jnp.bfloat16)
    return (attn_out, moe_out)


def solution(mesh):
    return jax.shard_map(
        local,
        mesh=mesh,
        in_specs=(
            P("req", "tp"),
            P(),
            P(None, "tp"),
            P(None, "tp"),
            P("tp"),
            P("req", "tp"),
            P("tp", None),
            P(),
            P("tp", None),
            P("req", None, None, "tp"),
            P("req", "tp", None),
            P("req", None),
            P(),
            P(),
        ),
        out_specs=(P("req", "tp"), P("req", "tp")),
        check_vma=False,
    )
```

```python
import functools

import jax
import jax.numpy as jnp
from jax import lax
from jax.experimental import pallas as pl
from jax.experimental.pallas import tpu as pltpu
from jax.sharding import PartitionSpec as P

D = 2880
HEAD = 64


rope_base = 150000.0
norm_eps = 1e-05
clamp_limit = 7.0
glu_alpha = 1.702


def rms_rows(values, gain):
    wide = values.astype(jnp.float32)
    factor = lax.rsqrt(jnp.mean(wide * wide, axis=1, keepdims=True) + norm_eps)
    return (wide * factor * gain).astype(jnp.bfloat16)


def rotate(values, positions):
    half_size = values.shape[-1] // 2
    powers = jnp.arange(half_size, dtype=jnp.float32) * (-2.0 / values.shape[-1])
    angles = positions[:, None, None] * rope_base**powers
    cosine = jnp.cos(angles)
    sine_part = jnp.sin(angles)
    first_half = values[..., :half_size]
    second_half = values[..., half_size:]
    return jnp.concatenate(
        [
            first_half * cosine - second_half * sine_part,
            second_half * cosine + first_half * sine_part,
        ],
        axis=-1,
    )


def flash_kernel(group_ref, q_ref, kv_ref, m0_ref, l0_ref, acc0_ref, out_ref, m_sc, l_sc, acc_sc, *, scale, steps):
    step = pl.program_id(1)

    @pl.when(step == 0)
    def _():
        m_sc[...] = m0_ref[...]
        l_sc[...] = l0_ref[...]
        acc_sc[...] = acc0_ref[...]

    block = kv_ref[...]
    scores = (
        lax.dot_general(
            q_ref[...], block, (((1,), (1,)), ((), ())), preferred_element_type=jnp.float32
        )
        * scale
    )
    m_prev = m_sc[...]
    m_new = jnp.maximum(m_prev, jnp.max(scores, axis=1, keepdims=True))
    weights = jnp.exp(scores - m_new)
    decay = jnp.exp(m_prev - m_new)
    l_sc[...] = decay * l_sc[...] + jnp.sum(weights, axis=1, keepdims=True)
    acc_sc[...] = decay * acc_sc[...] + jnp.dot(
        weights.astype(jnp.bfloat16), block, preferred_element_type=jnp.float32
    )
    m_sc[...] = m_new

    @pl.when(step == steps - 1)
    def _():
        out_ref[...] = (acc_sc[...] / l_sc[...]).astype(out_ref.dtype)


def prefix_attention(group, query, cache, peak, denominator, accum, *, prefix_len, scale):
    rows, width = query.shape
    block_q = min(rows, 1024)
    block_k = 4096
    steps = prefix_len // block_k
    grid = (rows // block_q, steps)
    kernel = functools.partial(flash_kernel, scale=scale, steps=steps)
    return pl.pallas_call(
        kernel,
        out_shape=jax.ShapeDtypeStruct((rows, width), jnp.bfloat16),
        grid_spec=pltpu.PrefetchScalarGridSpec(
            num_scalar_prefetch=1,
            grid=grid,
            in_specs=[
                pl.BlockSpec((block_q, width), lambda i, j, g: (i, 0)),
                pl.BlockSpec((block_k, width), lambda i, j, g: (g[0] * steps + j, 0)),
                pl.BlockSpec((block_q, 1), lambda i, j, g: (i, 0)),
                pl.BlockSpec((block_q, 1), lambda i, j, g: (i, 0)),
                pl.BlockSpec((block_q, width), lambda i, j, g: (i, 0)),
            ],
            out_specs=pl.BlockSpec((block_q, width), lambda i, j, g: (i, 0)),
            scratch_shapes=[
                pltpu.VMEM((block_q, 1), jnp.float32),
                pltpu.VMEM((block_q, 1), jnp.float32),
                pltpu.VMEM((block_q, width), jnp.float32),
            ],
        ),
        compiler_params=pltpu.CompilerParams(dimension_semantics=("arbitrary", "arbitrary")),
        cost_estimate=pl.CostEstimate(
            flops=4 * rows * prefix_len * width,
            transcendentals=rows * prefix_len,
            bytes_accessed=prefix_len * width * 2 + rows * width * 8,
        ),
    )(group, query, cache, peak, denominator, accum)


def local(
    hidden_states,
    attn_gain,
    query_weight,
    key_value_weight,
    sink_logits,
    prefix_cache,
    out_weight,
    ffn_gain,
    router_weight,
    gate_up_weight,
    down_weight,
    route_ids,
    prefix_group,
    suffix_lengths,
):
    token_count = hidden_states.shape[0]
    head_size = HEAD
    model_width = D
    local_heads = query_weight.shape[1] // head_size
    local_kv = key_value_weight.shape[1] // (2 * head_size)
    per_kv = local_heads // local_kv
    query_rows = per_kv * token_count
    req_count = lax.axis_size("req")
    req_index = lax.axis_index("req")
    tp_index = lax.axis_index("tp")
    cache_rows = prefix_cache.shape[0]
    prefix_len = cache_rows * req_count // 2
    score_scale = head_size ** (-0.5)
    col_count = hidden_states.shape[1]
    packed = jnp.concatenate([hidden_states.T, router_weight], axis=1)
    gathered = lax.all_gather(packed, "tp", axis=0, tiled=True)
    full_rows = gathered[:, :token_count].T
    router_full = gathered[:, token_count:]
    normed_attn = rms_rows(full_rows, attn_gain)
    positions = (prefix_len + jnp.arange(token_count, dtype=jnp.int32)).astype(jnp.float32)
    queries = jnp.dot(normed_attn, query_weight, preferred_element_type=jnp.float32)
    fresh = jnp.dot(normed_attn, key_value_weight, preferred_element_type=jnp.float32).reshape(
        token_count, local_kv, 2, head_size
    )
    queries = rotate(queries.reshape(token_count, local_heads, head_size), positions).astype(
        jnp.bfloat16
    )
    new_keys = rotate(fresh[:, :, 0], positions).astype(jnp.bfloat16)
    new_values = fresh[:, :, 1].astype(jnp.bfloat16)
    query_heads = (
        queries.reshape(token_count, local_kv, per_kv, head_size)
        .transpose(1, 2, 0, 3)
        .reshape(local_kv, query_rows, head_size)
    )
    assert local_kv == 1
    query_flat = query_heads.reshape(query_rows, head_size)
    fresh_kv = jnp.concatenate([new_keys[:, 0, :], new_values[:, 0, :]], axis=1)
    sink_rows = jnp.broadcast_to(
        sink_logits.reshape(per_kv, 1), (per_kv, token_count)
    ).reshape(query_rows, 1)
    row_pos = jnp.arange(query_rows, dtype=jnp.int32) % token_count
    causal = jnp.arange(token_count, dtype=jnp.int32)[None, :] <= row_pos[:, None]
    fresh_scores = (
        jnp.dot(query_flat, new_keys[:, 0, :].T, preferred_element_type=jnp.float32) * score_scale
    )
    fresh_scores = jnp.where(causal, fresh_scores, -jnp.inf)
    start_peak = jnp.maximum(sink_rows, jnp.max(fresh_scores, axis=1, keepdims=True))
    fresh_weights = jnp.exp(fresh_scores - start_peak)
    start_denominator = jnp.exp(sink_rows - start_peak) + jnp.sum(
        fresh_weights, axis=1, keepdims=True
    )
    start_accum = jnp.dot(
        fresh_weights.astype(jnp.bfloat16), fresh_kv, preferred_element_type=jnp.float32
    )
    query_padded = jnp.concatenate([query_flat, jnp.zeros_like(query_flat)], axis=1)
    own_group = prefix_group[req_index].reshape(1)
    shard_rows = lax.all_gather(prefix_cache, "req", axis=0, tiled=True)
    mixed_wide = prefix_attention(
        own_group, query_padded, shard_rows, start_peak, start_denominator, start_accum,
        prefix_len=prefix_len, scale=score_scale,
    )
    mixed = mixed_wide[:, head_size:].reshape(local_heads, token_count, head_size)
    attn_part = jnp.einsum(
        "hqd,hdo->qo",
        mixed,
        out_weight.reshape(local_heads, head_size, model_width),
        preferred_element_type=jnp.float32,
    )
    attn_sum = lax.psum_scatter(attn_part, "tp", scatter_dimension=1, tiled=True)
    live = (jnp.arange(token_count, dtype=jnp.int32) < suffix_lengths[req_index])[:, None]
    attn_out = jnp.where(live, attn_sum, 0.0).astype(jnp.bfloat16)
    expert_count = router_weight.shape[1]
    top_count = route_ids.shape[1]
    capacity = token_count * top_count * 3 // (2 * expert_count)
    entries = route_ids.reshape(-1)
    onehot = (entries[:, None] == jnp.arange(expert_count, dtype=jnp.int32)[None, :]).astype(
        jnp.int32
    )
    earlier = jnp.cumsum(onehot, axis=0) - onehot
    slots = jnp.sum(earlier * onehot, axis=1)
    targets = entries * capacity + slots
    sources = jnp.arange(token_count * top_count, dtype=jnp.int32) // top_count
    source_of = jnp.zeros((expert_count * capacity,), jnp.int32).at[targets].set(sources)
    filled = jnp.zeros((expert_count * capacity,), jnp.bool_).at[targets].set(True)
    exp_local = gate_up_weight.shape[0]
    ff_local = gate_up_weight.shape[3]
    joined_weight = gate_up_weight.reshape(exp_local, model_width, 2 * ff_local)
    resid = (hidden_states.astype(jnp.float32) + attn_sum).astype(jnp.bfloat16)
    resid_rows = lax.all_gather(resid, "tp", axis=1, tiled=True)
    normed_rows = rms_rows(resid_rows, ffn_gain)
    slot_hit = (
        targets.reshape(token_count, top_count)[:, :, None]
        == jnp.arange(expert_count * capacity, dtype=jnp.int32)[None, None, :]
    )
    token_slot = jnp.any(slot_hit, axis=1).astype(jnp.bfloat16)
    picked_rows = lax.dot_general(
        token_slot, normed_rows, (((0,), (0,)), ((), ())), preferred_element_type=jnp.float32
    ).astype(jnp.bfloat16)
    arrived = lax.all_to_all(
        picked_rows.reshape(expert_count, capacity, normed_rows.shape[1]),
        "req",
        split_axis=0,
        concat_axis=0,
        tiled=True,
    )
    item_count = arrived.shape[1]
    grouped = arrived.reshape(req_count, exp_local, item_count, model_width)
    projected = jnp.einsum(
        "sepd,edf->sepf", grouped, joined_weight, preferred_element_type=jnp.float32
    )
    gate_value = jnp.minimum(projected[..., :ff_local], clamp_limit)
    up_value = jnp.clip(projected[..., ff_local:], -clamp_limit, clamp_limit)
    active = ((up_value + 1.0) * gate_value * jax.nn.sigmoid(glu_alpha * gate_value)).astype(
        jnp.bfloat16
    )
    tp_count = lax.axis_size("tp")
    feat_part = model_width // tp_count
    send_results = jnp.einsum(
        "sepf,eftd->setpd",
        active,
        down_weight.reshape(exp_local, ff_local, tp_count, feat_part),
        preferred_element_type=jnp.float32,
    ).astype(jnp.bfloat16).reshape(req_count * exp_local * tp_count, item_count, feat_part)
    returned = lax.all_to_all(
        send_results, ("req", "tp"), split_axis=0, concat_axis=0, tiled=True
    )
    expert_parts = jnp.sum(
        returned.reshape(req_count * exp_local, tp_count, item_count, feat_part).astype(
            jnp.float32
        ),
        axis=1,
    )
    logits = jnp.dot(normed_rows, router_full, preferred_element_type=jnp.float32)
    chosen = jnp.take_along_axis(logits, route_ids, axis=1)
    raised = jnp.exp(chosen)
    gates = raised / jnp.sum(raised, axis=1, keepdims=True)
    gate_slot = jnp.sum(jnp.where(slot_hit, gates[:, :, None], 0.0), axis=1)
    moe_sum = jnp.dot(
        gate_slot,
        expert_parts.reshape(expert_count * capacity, feat_part),
        precision=lax.Precision.HIGHEST,
        preferred_element_type=jnp.float32,
    )
    moe_out = jnp.where(live, moe_sum, 0.0).astype(jnp.bfloat16)
    return (attn_out, moe_out)


def solution(mesh):
    return jax.shard_map(
        local,
        mesh=mesh,
        in_specs=(
            P("req", "tp"),
            P(),
            P(None, "tp"),
            P(None, "tp"),
            P("tp"),
            P("req", "tp"),
            P("tp", None),
            P(),
            P("tp", None),
            P("req", None, None, "tp"),
            P("req", "tp", None),
            P("req", None),
            P(),
            P(),
        ),
        out_specs=(P("req", "tp"), P("req", "tp")),
        check_vma=False,
    )
```

```python
import functools

import jax
import jax.numpy as jnp
from jax import lax
from jax.experimental import pallas as pl
from jax.experimental.pallas import tpu as pltpu
from jax.sharding import PartitionSpec as P

D = 2880
HEAD = 64


rope_base = 150000.0
norm_eps = 1e-05
clamp_limit = 7.0
glu_alpha = 1.702


def rms_rows(values, gain):
    wide = values.astype(jnp.float32)
    factor = lax.rsqrt(jnp.mean(wide * wide, axis=1, keepdims=True) + norm_eps)
    return (wide * factor * gain).astype(jnp.bfloat16)


def rotate(values, positions):
    half_size = values.shape[-1] // 2
    powers = jnp.arange(half_size, dtype=jnp.float32) * (-2.0 / values.shape[-1])
    angles = positions[:, None, None] * rope_base**powers
    cosine = jnp.cos(angles)
    sine_part = jnp.sin(angles)
    first_half = values[..., :half_size]
    second_half = values[..., half_size:]
    return jnp.concatenate(
        [
            first_half * cosine - second_half * sine_part,
            second_half * cosine + first_half * sine_part,
        ],
        axis=-1,
    )


def flash_kernel(group_ref, q_ref, kv_ref, m0_ref, l0_ref, acc0_ref, out_ref, m_sc, l_sc, acc_sc, *, scale, steps):
    step = pl.program_id(1)

    @pl.when(step == 0)
    def _():
        m_sc[...] = m0_ref[...]
        l_sc[...] = l0_ref[...]
        acc_sc[...] = acc0_ref[...]

    block = kv_ref[...]
    scores = (
        lax.dot_general(
            q_ref[...], block, (((1,), (1,)), ((), ())), preferred_element_type=jnp.float32
        )
        * scale
    )
    m_prev = m_sc[...]
    m_new = jnp.maximum(m_prev, jnp.max(scores, axis=1, keepdims=True))
    weights = jnp.exp(scores - m_new)
    decay = jnp.exp(m_prev - m_new)
    l_sc[...] = decay * l_sc[...] + jnp.sum(weights, axis=1, keepdims=True)
    acc_sc[...] = decay * acc_sc[...] + jnp.dot(
        weights.astype(jnp.bfloat16), block, preferred_element_type=jnp.float32
    )
    m_sc[...] = m_new

    @pl.when(step == steps - 1)
    def _():
        out_ref[...] = (acc_sc[...] / l_sc[...]).astype(out_ref.dtype)


def prefix_attention(group, query, cache, peak, denominator, accum, *, prefix_len, scale):
    rows, width = query.shape
    block_q = min(rows, 1024)
    block_k = 4096
    steps = prefix_len // block_k
    grid = (rows // block_q, steps)
    kernel = functools.partial(flash_kernel, scale=scale, steps=steps)
    return pl.pallas_call(
        kernel,
        out_shape=jax.ShapeDtypeStruct((rows, width), jnp.bfloat16),
        grid_spec=pltpu.PrefetchScalarGridSpec(
            num_scalar_prefetch=1,
            grid=grid,
            in_specs=[
                pl.BlockSpec((block_q, width), lambda i, j, g: (i, 0)),
                pl.BlockSpec((block_k, width), lambda i, j, g: (g[0] * steps + j, 0)),
                pl.BlockSpec((block_q, 1), lambda i, j, g: (i, 0)),
                pl.BlockSpec((block_q, 1), lambda i, j, g: (i, 0)),
                pl.BlockSpec((block_q, width), lambda i, j, g: (i, 0)),
            ],
            out_specs=pl.BlockSpec((block_q, width), lambda i, j, g: (i, 0)),
            scratch_shapes=[
                pltpu.VMEM((block_q, 1), jnp.float32),
                pltpu.VMEM((block_q, 1), jnp.float32),
                pltpu.VMEM((block_q, width), jnp.float32),
            ],
        ),
        compiler_params=pltpu.CompilerParams(dimension_semantics=("arbitrary", "arbitrary")),
        cost_estimate=pl.CostEstimate(
            flops=4 * rows * prefix_len * width,
            transcendentals=rows * prefix_len,
            bytes_accessed=prefix_len * width * 2 + rows * width * 8,
        ),
    )(group, query, cache, peak, denominator, accum)


def local(
    hidden_states,
    attn_gain,
    query_weight,
    key_value_weight,
    sink_logits,
    prefix_cache,
    out_weight,
    ffn_gain,
    router_weight,
    gate_up_weight,
    down_weight,
    route_ids,
    prefix_group,
    suffix_lengths,
):
    token_count = hidden_states.shape[0]
    head_size = HEAD
    model_width = D
    local_heads = query_weight.shape[1] // head_size
    local_kv = key_value_weight.shape[1] // (2 * head_size)
    per_kv = local_heads // local_kv
    query_rows = per_kv * token_count
    req_count = lax.axis_size("req")
    req_index = lax.axis_index("req")
    tp_index = lax.axis_index("tp")
    cache_rows = prefix_cache.shape[0]
    prefix_len = cache_rows * req_count // 2
    score_scale = head_size ** (-0.5)
    col_count = hidden_states.shape[1]
    packed = jnp.concatenate([hidden_states.T, router_weight], axis=1)
    gathered = lax.all_gather(packed, "tp", axis=0, tiled=True)
    full_rows = gathered[:, :token_count].T
    router_full = gathered[:, token_count:]
    normed_attn = rms_rows(full_rows, attn_gain)
    positions = (prefix_len + jnp.arange(token_count, dtype=jnp.int32)).astype(jnp.float32)
    queries = jnp.dot(normed_attn, query_weight, preferred_element_type=jnp.float32)
    fresh = jnp.dot(normed_attn, key_value_weight, preferred_element_type=jnp.float32).reshape(
        token_count, local_kv, 2, head_size
    )
    queries = rotate(queries.reshape(token_count, local_heads, head_size), positions).astype(
        jnp.bfloat16
    )
    new_keys = rotate(fresh[:, :, 0], positions).astype(jnp.bfloat16)
    new_values = fresh[:, :, 1].astype(jnp.bfloat16)
    query_heads = (
        queries.reshape(token_count, local_kv, per_kv, head_size)
        .transpose(1, 2, 0, 3)
        .reshape(local_kv, query_rows, head_size)
    )
    assert local_kv == 1
    query_flat = query_heads.reshape(query_rows, head_size)
    fresh_kv = jnp.concatenate([new_keys[:, 0, :], new_values[:, 0, :]], axis=1)
    sink_rows = jnp.broadcast_to(
        sink_logits.reshape(per_kv, 1), (per_kv, token_count)
    ).reshape(query_rows, 1)
    row_pos = jnp.arange(query_rows, dtype=jnp.int32) % token_count
    causal = jnp.arange(token_count, dtype=jnp.int32)[None, :] <= row_pos[:, None]
    fresh_scores = (
        jnp.dot(query_flat, new_keys[:, 0, :].T, preferred_element_type=jnp.float32) * score_scale
    )
    fresh_scores = jnp.where(causal, fresh_scores, -jnp.inf)
    start_peak = jnp.maximum(sink_rows, jnp.max(fresh_scores, axis=1, keepdims=True))
    fresh_weights = jnp.exp(fresh_scores - start_peak)
    start_denominator = jnp.exp(sink_rows - start_peak) + jnp.sum(
        fresh_weights, axis=1, keepdims=True
    )
    start_accum = jnp.dot(
        fresh_weights.astype(jnp.bfloat16), fresh_kv, preferred_element_type=jnp.float32
    )
    query_padded = jnp.concatenate([query_flat, jnp.zeros_like(query_flat)], axis=1)
    own_group = prefix_group[req_index].reshape(1)
    shard_rows = lax.all_gather(prefix_cache, "req", axis=0, tiled=True)
    mixed_wide = prefix_attention(
        own_group, query_padded, shard_rows, start_peak, start_denominator, start_accum,
        prefix_len=prefix_len, scale=score_scale,
    )
    mixed = mixed_wide[:, head_size:].reshape(local_heads, token_count, head_size)
    attn_part = jnp.einsum(
        "hqd,hdo->qo",
        mixed,
        out_weight.reshape(local_heads, head_size, model_width),
        preferred_element_type=jnp.float32,
    )
    attn_sum = lax.psum_scatter(attn_part, "tp", scatter_dimension=1, tiled=True)
    live = (jnp.arange(token_count, dtype=jnp.int32) < suffix_lengths[req_index])[:, None]
    attn_out = jnp.where(live, attn_sum, 0.0).astype(jnp.bfloat16)
    expert_count = router_weight.shape[1]
    top_count = route_ids.shape[1]
    capacity = token_count * top_count * 3 // (2 * expert_count)
    entries = route_ids.reshape(-1)
    onehot = (entries[:, None] == jnp.arange(expert_count, dtype=jnp.int32)[None, :]).astype(
        jnp.int32
    )
    earlier = jnp.cumsum(onehot, axis=0) - onehot
    slots = jnp.sum(earlier * onehot, axis=1)
    targets = entries * capacity + slots
    sources = jnp.arange(token_count * top_count, dtype=jnp.int32) // top_count
    source_of = jnp.zeros((expert_count * capacity,), jnp.int32).at[targets].set(sources)
    filled = jnp.zeros((expert_count * capacity,), jnp.bool_).at[targets].set(True)
    exp_local = gate_up_weight.shape[0]
    ff_local = gate_up_weight.shape[3]
    joined_weight = gate_up_weight.reshape(exp_local, model_width, 2 * ff_local)
    resid = (hidden_states.astype(jnp.float32) + attn_sum).astype(jnp.bfloat16)
    resid_rows = lax.all_gather(resid, "tp", axis=1, tiled=True)
    normed_rows = rms_rows(resid_rows, ffn_gain)
    slot_hit = (
        targets.reshape(token_count, top_count)[:, :, None]
        == jnp.arange(expert_count * capacity, dtype=jnp.int32)[None, None, :]
    )
    token_slot = jnp.any(slot_hit, axis=1).astype(jnp.bfloat16)
    picked_rows = lax.dot_general(
        token_slot, normed_rows, (((0,), (0,)), ((), ())), preferred_element_type=jnp.float32
    ).astype(jnp.bfloat16)
    arrived = lax.all_to_all(
        picked_rows.reshape(expert_count, capacity, normed_rows.shape[1]),
        "req",
        split_axis=0,
        concat_axis=0,
        tiled=True,
    )
    item_count = arrived.shape[1]
    grouped = arrived.reshape(req_count, exp_local, item_count, model_width)
    projected = jnp.einsum(
        "sepd,edf->sepf", grouped, joined_weight, preferred_element_type=jnp.float32
    )
    gate_value = jnp.minimum(projected[..., :ff_local], clamp_limit)
    up_value = jnp.clip(projected[..., ff_local:], -clamp_limit, clamp_limit)
    active = ((up_value + 1.0) * gate_value * jax.nn.sigmoid(glu_alpha * gate_value)).astype(
        jnp.bfloat16
    )
    tp_count = lax.axis_size("tp")
    feat_part = model_width // tp_count
    send_results = jnp.einsum(
        "sepf,eftd->setpd",
        active,
        down_weight.reshape(exp_local, ff_local, tp_count, feat_part),
        preferred_element_type=jnp.float32,
    ).astype(jnp.bfloat16).reshape(req_count * exp_local * tp_count, item_count, feat_part)
    returned = lax.all_to_all(
        send_results, ("req", "tp"), split_axis=0, concat_axis=0, tiled=True
    )
    logits = jnp.dot(normed_rows, router_full, preferred_element_type=jnp.float32)
    chosen = jnp.take_along_axis(logits, route_ids, axis=1)
    raised = jnp.exp(chosen)
    gates = raised / jnp.sum(raised, axis=1, keepdims=True)
    gate_slot = jnp.sum(jnp.where(slot_hit, gates[:, :, None], 0.0), axis=1)
    gate_parts = jnp.broadcast_to(
        gate_slot.reshape(token_count, req_count * exp_local, 1, item_count),
        (token_count, req_count * exp_local, tp_count, item_count),
    ).reshape(token_count, req_count * exp_local * tp_count * item_count)
    moe_sum = jnp.dot(
        gate_parts,
        returned.reshape(req_count * exp_local * tp_count * item_count, feat_part).astype(
            jnp.float32
        ),
        precision=lax.Precision.HIGHEST,
        preferred_element_type=jnp.float32,
    )
    moe_out = jnp.where(live, moe_sum, 0.0).astype(jnp.bfloat16)
    return (attn_out, moe_out)


def solution(mesh):
    return jax.shard_map(
        local,
        mesh=mesh,
        in_specs=(
            P("req", "tp"),
            P(),
            P(None, "tp"),
            P(None, "tp"),
            P("tp"),
            P("req", "tp"),
            P("tp", None),
            P(),
            P("tp", None),
            P("req", None, None, "tp"),
            P("req", "tp", None),
            P("req", None),
            P(),
            P(),
        ),
        out_specs=(P("req", "tp"), P("req", "tp")),
        check_vma=False,
    )
```
